32 devices in a mesh: dp: 4 (over x, core), expert: 8 (over z, y).
Axes of the slice: x: 2, y: 2, z: 4, core: 2. Of those that a mesh axis runs over, the one named last changes fastest.
Arguments:
- latents: bfloat16 [16384, 768], P(('dp', 'expert')), may hold values from -6 to 6
- cotangent: bfloat16 [16384, 768], P(('dp', 'expert')), may hold values from -6 to 6
- expert_of_row: int32 [16384], P(('dp', 'expert')), may hold values from 0 to 7, as said below
- w_in: bfloat16 [8, 768, 1536], P('expert'), may hold values from -0.21875 to 0.21875
- w_out: bfloat16 [8, 1536, 768], P('expert'), may hold values from -0.15625 to 0.15625
Outputs:
- grad_latents: bfloat16 [16384, 768], P(('dp', 'expert'))
- grad_w_in: float32 [8, 768, 1536], P('expert', 'dp')
- grad_w_out: float32 [8, 1536, 768], P('expert', 'dp')
The draws below stay inside these ranges and needn't reach their ends.
Inputs may be any that keep to these rules, and one draw needn't show every extreme that they name: `expert_of_row`: in every aligned block of 512 rows (the rows of one device) each expert is named by at most 96 rows, and one expert, the same for all blocks, is named by exactly 96 rows in every block.
All inputs are finite; a program needn't handle non-finite values.
Results may differ from the reference program's by a relative error of at most 0.008.
Values may be sent and summed in bfloat16 or wider, within the bound.
No kernel may reach another device: no remote copies, remote signals or barrier semaphores. Data moves between devices by JAX's collectives and lax.ppermute only.
A program may use at most 64 MiB of HBM per device.

```python
import math
import jax
import jax.numpy as jnp
from jax import lax

D = 768
FF = 1536
TOK_DEV = 512
EXPERTS = 8
CAP = 96
TOKENS = 16384
N_DP = 4
N_EXPERT = 8


def draw_expert_of_row(key, part):
    blocks = TOKENS // TOK_DEV
    hottest = jax.random.randint(jax.random.fold_in(key, 7), (), 0, EXPERTS).astype(jnp.int32)
    leaning = jax.random.randint(jax.random.fold_in(key, 11), (EXPERTS,), 1, 9).astype(jnp.int32)
    others = jnp.arange(EXPERTS - 1, dtype=jnp.int32)
    others = others + (others >= hottest).astype(jnp.int32)
    owners = jnp.repeat(others, CAP, total_repeat_length=(EXPERTS - 1) * CAP)
    positions = jnp.arange((EXPERTS - 1) * CAP, dtype=jnp.int32)

    def one_block(index):
        block_key = jax.random.fold_in(key, 1000 + index)
        noise = jax.random.randint(jax.random.fold_in(block_key, 1), owners.shape, 0, 4096).astype(jnp.int32)
        score = noise * leaning[owners] * 4096 + positions
        _, chosen = lax.top_k(score, TOK_DEV - CAP)
        picked = owners[chosen]
        listing = jnp.concatenate([jnp.full((CAP,), hottest, jnp.int32), picked])
        return jax.random.permutation(jax.random.fold_in(block_key, 2), listing)
    return jax.vmap(one_block)(jnp.arange(blocks, dtype=jnp.int32)).reshape(TOKENS).astype(jnp.int32)


def shard_levels(rng, dims, shards, smallest, high):
    def one(position, parts):
        heights = jax.random.uniform(jax.random.fold_in(jax.random.fold_in(rng, 6), position), (parts,), jnp.float32, smallest / len(shards), high / len(shards))
        return jnp.repeat(jnp.exp(heights), dims[position] // parts).reshape((-1,) + (1,) * (len(dims) - position - 1))

    level = one(*shards[0])
    for cut in shards[1:]:
        level = level * one(*cut)
    return level


def bell_draw(rng, dims, scale, bound, cuts=(), held_as=jnp.bfloat16):
    array = jax.random.normal(rng, dims, jnp.float32) * scale
    if len(cuts) > 0:
        array = shard_levels(rng, dims, cuts, -0.22, 0.18) * array
    return jnp.clip(array, min=-bound, max=bound).astype(held_as)


def setup_inputs(seed: int = 0) -> dict:
    arg_keys = jax.random.split(jax.random.key(seed), 6)
    return {
        "latents": bell_draw(arg_keys[0], (TOKENS, D), 1.0, 6.0, ((0, 32),)),
        "cotangent": bell_draw(arg_keys[1], (TOKENS, D), 1.0, 6.0, ((0, 32),)),
        "expert_of_row": draw_expert_of_row(jax.random.fold_in(arg_keys[5], 71), 0),
        "w_in": bell_draw(arg_keys[3], (EXPERTS, D, FF), D ** -0.5, 0.21875, ((0, 8),)),
        "w_out": bell_draw(arg_keys[4], (EXPERTS, FF, D), FF ** -0.5, 0.15625, ((0, 8),)),
    }


def gelu_parts(value):
    coeff = 0.7978845608028654
    cube = value * value * value
    inner = jnp.tanh(coeff * (value + 0.044715 * cube))
    result = 0.5 * value * (1.0 + inner)
    slope = 0.5 * (1.0 + inner) + 0.5 * value * (1.0 - inner * inner) * coeff * (1.0 + 3.0 * 0.044715 * value * value)
    return (result, slope)

def reference(latents, cotangent, expert_of_row, w_in, w_out):
    groups = TOKENS // (N_EXPERT * TOK_DEV)
    slots = N_EXPERT * CAP
    route = expert_of_row.reshape(groups, N_EXPERT, TOK_DEV)
    member = (route[..., None] == jnp.arange(EXPERTS, dtype=jnp.int32)).astype(jnp.int32)
    before = jnp.cumsum(member, axis=2, dtype=jnp.int32) - member
    rank = lax.optimization_barrier(jnp.sum(before * member, axis=3, dtype=jnp.int32))
    source = jnp.arange(N_EXPERT, dtype=jnp.int32)[None, :, None]
    target = (route * slots + source * CAP + rank).astype(jnp.int32).reshape(groups, N_EXPERT * TOK_DEV)
    stacked = jnp.concatenate([latents, cotangent], axis=1).reshape(groups, N_EXPERT * TOK_DEV, 2 * D)
    scale = 1.0 / math.sqrt(N_DP * TOK_DEV)

    def one_expert(piece):
        block, first, second = piece
        inputs = block[:, :D]
        grads = block[:, D:]
        pre_act = jnp.dot(inputs, first, preferred_element_type=jnp.float32)
        value, slope = gelu_parts(pre_act)
        act = value.astype(jnp.bfloat16)
        act_grad = jnp.dot(grads, second.T, preferred_element_type=jnp.float32)
        hidden_grad = (act_grad * slope).astype(jnp.bfloat16)
        row_grad = jnp.dot(hidden_grad, first.T, preferred_element_type=jnp.float32).astype(jnp.bfloat16)
        part_in = (scale * jnp.dot(inputs.T, hidden_grad, preferred_element_type=jnp.float32)).astype(jnp.bfloat16)
        part_out = (scale * jnp.dot(act.T, grads, preferred_element_type=jnp.float32)).astype(jnp.bfloat16)
        return (row_grad, part_in, part_out)

    def one_group(carry, item):
        index, rows_in = item
        buffer = jnp.zeros((EXPERTS * slots, 2 * D), jnp.bfloat16).at[index].set(rows_in)
        buffer = buffer.reshape(EXPERTS, slots, 2 * D)
        row_grad, part_in, part_out = lax.map(one_expert, (buffer, w_in, w_out))
        rows_back = row_grad.reshape(EXPERTS * slots, D)[index]
        return ((carry[0] + part_in.astype(jnp.float32), carry[1] + part_out.astype(jnp.float32)), rows_back)
    start = (jnp.zeros((EXPERTS, D, FF), jnp.float32), jnp.zeros((EXPERTS, FF, D), jnp.float32))
    (grad_w_in, grad_w_out), rows_all = lax.scan(one_group, start, (target, stacked))
    return (rows_all.reshape(TOKENS, D), grad_w_in, grad_w_out)
```

```python
import math

import jax
import jax.numpy as jnp
from jax import lax
from jax.sharding import PartitionSpec as P


def gelu_parts(value):
    coeff = 0.7978845608028654
    cube = value * value * value
    inner = jnp.tanh(coeff * (value + 0.044715 * cube))
    result = 0.5 * value * (1.0 + inner)
    slope = 0.5 * (1.0 + inner) + 0.5 * value * (1.0 - inner * inner) * coeff * (
        1.0 + 3.0 * 0.044715 * value * value
    )
    return (result, slope)


def block_pass(block, w_first, w_second):
    width = block.shape[1] // 2
    inputs = block[:, :width]
    grads = block[:, width:]
    pre_act = jnp.dot(inputs, w_first, preferred_element_type=jnp.float32)
    value, slope = gelu_parts(pre_act)
    act = value.astype(jnp.bfloat16)
    act_grad = lax.dot_general(
        grads, w_second, (((1,), (1,)), ((), ())), preferred_element_type=jnp.float32
    )
    hidden_grad = (act_grad * slope).astype(jnp.bfloat16)
    row_grad = lax.dot_general(
        hidden_grad, w_first, (((1,), (1,)), ((), ())), preferred_element_type=jnp.float32
    ).astype(jnp.bfloat16)
    return row_grad, act, hidden_grad


def weight_parts(blocks, acts, hidden_grads):
    width = blocks[0].shape[1] // 2
    block = jnp.concatenate(blocks, axis=0)
    act = jnp.concatenate(acts, axis=0)
    hidden_grad = jnp.concatenate(hidden_grads, axis=0)
    part_in = lax.dot_general(
        block[:, :width], hidden_grad, (((0,), (0,)), ((), ())),
        preferred_element_type=jnp.float32,
    )
    part_out = lax.dot_general(
        act, block[:, width:], (((0,), (0,)), ((), ())), preferred_element_type=jnp.float32
    )
    return part_in, part_out


def per_device(latents, cotangent, expert_of_row, w_in, w_out):
    rows, width = latents.shape
    experts = lax.axis_size("expert")
    groups = lax.axis_size("dp")
    capacity = 3 * rows // (2 * experts)
    slots = experts * capacity
    me = lax.axis_index("expert")
    relative = (expert_of_row - me + experts) % experts
    member = (relative[:, None] == jnp.arange(experts, dtype=jnp.int32)[None, :]).astype(
        jnp.int32
    )
    before = jnp.cumsum(member, axis=0, dtype=jnp.int32) - member
    rank = jnp.sum(before * member, axis=1, dtype=jnp.int32)
    slot = relative * capacity + rank
    stacked = jnp.concatenate([latents, cotangent], axis=1)
    table = (slot[None, :] == jnp.arange(slots, dtype=jnp.int32)[:, None]).astype(jnp.bfloat16)
    outgoing = jnp.dot(table, stacked, preferred_element_type=jnp.float32).astype(jnp.bfloat16)
    outgoing = outgoing.reshape(experts, capacity, 2 * width)
    w_first = w_in[0]
    w_second = w_out[0]

    returned = []
    part_in = None
    part_out = None
    chunks = 2
    per_chunk = experts // chunks
    for chunk in range(chunks):
        blocks, acts, hidden_grads = [], [], []
        for shift in range(chunk * per_chunk, (chunk + 1) * per_chunk):
            block = outgoing[shift]
            if shift:
                block = lax.ppermute(
                    block, "expert", [(j, (j + shift) % experts) for j in range(experts)]
                )
            row_grad, act, hidden_grad = block_pass(block, w_first, w_second)
            if shift:
                row_grad = lax.ppermute(
                    row_grad, "expert", [((j + shift) % experts, j) for j in range(experts)]
                )
            returned.append(row_grad)
            blocks.append(block)
            acts.append(act)
            hidden_grads.append(hidden_grad)
        p_in, p_out = weight_parts(blocks, acts, hidden_grads)
        part_in = p_in if part_in is None else part_in + p_in
        part_out = p_out if part_out is None else part_out + p_out

    scale = 1.0 / math.sqrt(groups * rows)
    grad_w_in = lax.psum_scatter(
        (scale * part_in).astype(jnp.bfloat16), "dp", scatter_dimension=0, tiled=True
    ).astype(jnp.float32)
    grad_w_out = lax.psum_scatter(
        (scale * part_out).astype(jnp.bfloat16), "dp", scatter_dimension=0, tiled=True
    ).astype(jnp.float32)
    returned = jnp.concatenate(returned, axis=0)
    grad_latents = lax.dot_general(
        table, returned, (((0,), (0,)), ((), ())), preferred_element_type=jnp.float32
    )
    grad_latents = grad_latents.astype(jnp.bfloat16)
    return (grad_latents, grad_w_in[None], grad_w_out[None])


def solution(mesh):
    return jax.shard_map(
        per_device,
        mesh=mesh,
        in_specs=(
            P(("dp", "expert"), None),
            P(("dp", "expert"), None),
            P(("dp", "expert")),
            P("expert", None, None),
            P("expert", None, None),
        ),
        out_specs=(P(("dp", "expert"), None), P("expert", "dp", None), P("expert", "dp", None)),
        check_vma=False,
    )
```

```python
import math

import jax
import jax.numpy as jnp
from jax import lax
from jax.sharding import PartitionSpec as P

CHUNKS = 3


def gelu_parts(value):
    coeff = 0.7978845608028654
    cube = value * value * value
    inner = jnp.tanh(coeff * (value + 0.044715 * cube))
    result = 0.5 * value * (1.0 + inner)
    slope = 0.5 * (1.0 + inner) + 0.5 * value * (1.0 - inner * inner) * coeff * (
        1.0 + 3.0 * 0.044715 * value * value
    )
    return (result, slope)


def block_pass(block, w_first, w_second):
    width = block.shape[1] // 2
    inputs = block[:, :width]
    grads = block[:, width:]
    pre_act = jnp.dot(inputs, w_first, preferred_element_type=jnp.float32)
    value, slope = gelu_parts(pre_act)
    act = value.astype(jnp.bfloat16)
    act_grad = lax.dot_general(
        grads, w_second, (((1,), (1,)), ((), ())), preferred_element_type=jnp.float32
    )
    hidden_grad = (act_grad * slope).astype(jnp.bfloat16)
    row_grad = lax.dot_general(
        hidden_grad, w_first, (((1,), (1,)), ((), ())), preferred_element_type=jnp.float32
    ).astype(jnp.bfloat16)
    return row_grad, act, hidden_grad


def reduce_scatter_dp(partial, groups):
    index = lax.axis_index("dp")
    levels = groups.bit_length() - 1
    rows = partial.shape[0] // groups
    blocks = partial.reshape((2,) * levels + (rows,) + partial.shape[1:])
    for level in range(levels):
        axis = levels - 1 - level
        bit = (index >> level) & 1
        keep = lax.dynamic_index_in_dim(blocks, bit, axis, keepdims=False)
        send = lax.dynamic_index_in_dim(blocks, 1 - bit, axis, keepdims=False)
        got = lax.ppermute(
            send.astype(jnp.bfloat16), "dp", [(j, j ^ (1 << level)) for j in range(groups)]
        )
        blocks = keep + got.astype(jnp.float32)
    return blocks


def per_device(latents, cotangent, expert_of_row, w_in, w_out):
    rows, width = latents.shape
    experts = lax.axis_size("expert")
    groups = lax.axis_size("dp")
    capacity = 3 * rows // (2 * experts)
    slots = experts * capacity
    me = lax.axis_index("expert")
    relative = (expert_of_row - me + experts) % experts
    member = (relative[:, None] == jnp.arange(experts, dtype=jnp.int32)[None, :]).astype(
        jnp.int32
    )
    before = jnp.cumsum(member, axis=0, dtype=jnp.int32) - member
    rank = jnp.sum(before * member, axis=1, dtype=jnp.int32)
    slot = relative * capacity + rank
    stacked = jnp.concatenate([latents, cotangent], axis=1)
    table = (slot[None, :] == jnp.arange(slots, dtype=jnp.int32)[:, None]).astype(jnp.bfloat16)
    outgoing = jnp.dot(table, stacked, preferred_element_type=jnp.float32).astype(jnp.bfloat16)
    outgoing = outgoing.reshape(experts, capacity, 2 * width)
    w_first = w_in[0]
    w_second = w_out[0]

    chunks = CHUNKS if capacity % CHUNKS == 0 else 1
    piece = capacity // chunks
    local = outgoing[0]
    local_grad, act, hidden_grad = block_pass(local, w_first, w_second)
    part_in = lax.dot_general(
        local[:, :width], hidden_grad, (((0,), (0,)), ((), ())),
        preferred_element_type=jnp.float32,
    )
    part_out = lax.dot_general(
        act, local[:, width:], (((0,), (0,)), ((), ())), preferred_element_type=jnp.float32
    )
    back = [[None] * chunks for _ in range(experts)]

    def dispatch(chunk):
        sending = outgoing[1:, chunk * piece:(chunk + 1) * piece]
        return [
            lax.ppermute(
                sending[shift - 1], "expert", [(j, (j + shift) % experts) for j in range(experts)]
            )
            for shift in range(1, experts)
        ]

    arrived = dispatch(0)
    for chunk in range(chunks):
        block = jnp.concatenate(arrived, axis=0)
        if chunk + 1 < chunks:
            later = outgoing[1:, (chunk + 1) * piece:(chunk + 2) * piece]
            later, block = lax.optimization_barrier((later, block))
            arrived = [
                lax.ppermute(
                    later[shift - 1], "expert",
                    [(j, (j + shift) % experts) for j in range(experts)],
                )
                for shift in range(1, experts)
            ]
        row_grad, act, hidden_grad = block_pass(block, w_first, w_second)
        if chunk + 1 < chunks:
            arrived, _ = lax.optimization_barrier((arrived, row_grad))
        part_in = part_in + lax.dot_general(
            block[:, :width], hidden_grad, (((0,), (0,)), ((), ())),
            preferred_element_type=jnp.float32,
        )
        part_out = part_out + lax.dot_general(
            act, block[:, width:], (((0,), (0,)), ((), ())), preferred_element_type=jnp.float32
        )
        for shift in range(1, experts):
            back[shift][chunk] = lax.ppermute(
                row_grad[(shift - 1) * piece:shift * piece],
                "expert",
                [((j + shift) % experts, j) for j in range(experts)],
            )
    pieces = [local_grad]
    for shift in range(1, experts):
        pieces.extend(back[shift])
    returned = jnp.concatenate(pieces, axis=0)

    scale = 1.0 / math.sqrt(groups * rows)
    grad_w_in = reduce_scatter_dp(scale * part_in, groups)
    grad_w_out = reduce_scatter_dp(scale * part_out, groups)
    grad_latents = lax.dot_general(
        table, returned, (((0,), (0,)), ((), ())), preferred_element_type=jnp.float32
    )
    grad_latents = grad_latents.astype(jnp.bfloat16)
    return (grad_latents, grad_w_in[None], grad_w_out[None])


def solution(mesh):
    return jax.shard_map(
        per_device,
        mesh=mesh,
        in_specs=(
            P(("dp", "expert"), None),
            P(("dp", "expert"), None),
            P(("dp", "expert")),
            P("expert", None, None),
            P("expert", None, None),
        ),
        out_specs=(P(("dp", "expert"), None), P("expert", "dp", None), P("expert", "dp", None)),
        check_vma=False,
    )
```

```python
import math

import jax
import jax.numpy as jnp
from jax import lax
from jax.sharding import PartitionSpec as P


def gelu_parts(value):
    coeff = 0.7978845608028654
    cube = value * value * value
    inner = jnp.tanh(coeff * (value + 0.044715 * cube))
    result = 0.5 * value * (1.0 + inner)
    slope = 0.5 * (1.0 + inner) + 0.5 * value * (1.0 - inner * inner) * coeff * (
        1.0 + 3.0 * 0.044715 * value * value
    )
    return (result, slope)


def block_pass(block, w_first, w_second):
    width = block.shape[1] // 2
    inputs = block[:, :width]
    grads = block[:, width:]
    pre_act = jnp.dot(inputs, w_first, preferred_element_type=jnp.float32)
    value, slope = gelu_parts(pre_act)
    act = value.astype(jnp.bfloat16)
    act_grad = lax.dot_general(
        grads, w_second, (((1,), (1,)), ((), ())), preferred_element_type=jnp.float32
    )
    hidden_grad = (act_grad * slope).astype(jnp.bfloat16)
    row_grad = lax.dot_general(
        hidden_grad, w_first, (((1,), (1,)), ((), ())), preferred_element_type=jnp.float32
    ).astype(jnp.bfloat16)
    return row_grad, act, hidden_grad


def weight_parts(blocks, acts, hidden_grads):
    width = blocks[0].shape[1] // 2
    block = jnp.concatenate(blocks, axis=0)
    act = jnp.concatenate(acts, axis=0)
    hidden_grad = jnp.concatenate(hidden_grads, axis=0)
    part_in = lax.dot_general(
        block[:, :width], hidden_grad, (((0,), (0,)), ((), ())),
        preferred_element_type=jnp.float32,
    )
    part_out = lax.dot_general(
        act, block[:, width:], (((0,), (0,)), ((), ())), preferred_element_type=jnp.float32
    )
    return part_in, part_out


def reduce_scatter_dp(partial, groups):
    index = lax.axis_index("dp")
    levels = groups.bit_length() - 1
    rows = partial.shape[0] // groups
    blocks = partial.reshape((2,) * levels + (rows,) + partial.shape[1:])
    for level in range(levels):
        axis = levels - 1 - level
        bit = (index >> level) & 1
        keep = lax.dynamic_index_in_dim(blocks, bit, axis, keepdims=False)
        send = lax.dynamic_index_in_dim(blocks, 1 - bit, axis, keepdims=False)
        got = lax.ppermute(
            send.astype(jnp.bfloat16), "dp", [(j, j ^ (1 << level)) for j in range(groups)]
        )
        blocks = keep + got.astype(jnp.float32)
    return blocks


def per_device(latents, cotangent, expert_of_row, w_in, w_out):
    rows, width = latents.shape
    experts = lax.axis_size("expert")
    groups = lax.axis_size("dp")
    capacity = 3 * rows // (2 * experts)
    slots = experts * capacity
    me = lax.axis_index("expert")
    relative = (expert_of_row - me + experts) % experts
    member = (relative[:, None] == jnp.arange(experts, dtype=jnp.int32)[None, :]).astype(
        jnp.int32
    )
    before = jnp.cumsum(member, axis=0, dtype=jnp.int32) - member
    rank = jnp.sum(before * member, axis=1, dtype=jnp.int32)
    slot = relative * capacity + rank
    stacked = jnp.concatenate([latents, cotangent], axis=1)
    table = (slot[None, :] == jnp.arange(slots, dtype=jnp.int32)[:, None]).astype(jnp.bfloat16)
    outgoing = jnp.dot(table, stacked, preferred_element_type=jnp.float32).astype(jnp.bfloat16)
    outgoing = outgoing.reshape(experts, capacity, 2 * width)
    w_first = w_in[0]
    w_second = w_out[0]

    arrived = [outgoing[0]] + [
        lax.ppermute(
            outgoing[shift], "expert", [(j, (j + shift) % experts) for j in range(experts)]
        )
        for shift in range(1, experts)
    ]
    lag = 2
    split = experts // 2
    back = [None] * experts
    acts, hidden_grads = [], []
    part_in = None
    part_out = None
    for shift in range(experts):
        block = arrived[shift]
        if shift >= lag + 1:
            block, _ = lax.optimization_barrier((block, back[shift - lag]))
            arrived[shift] = block
        row_grad, act, hidden_grad = block_pass(block, w_first, w_second)
        acts.append(act)
        hidden_grads.append(hidden_grad)
        if shift:
            back[shift] = lax.ppermute(
                row_grad, "expert", [((j + shift) % experts, j) for j in range(experts)]
            )
        else:
            back[shift] = row_grad
        if shift + 1 in (split, experts):
            first = 0 if shift + 1 == split else split
            p_in, p_out = weight_parts(
                arrived[first:shift + 1], acts[first:shift + 1], hidden_grads[first:shift + 1]
            )
            part_in = p_in if part_in is None else part_in + p_in
            part_out = p_out if part_out is None else part_out + p_out
    returned = jnp.concatenate(back, axis=0)

    scale = 1.0 / math.sqrt(groups * rows)
    grad_w_in = reduce_scatter_dp(scale * part_in, groups)
    grad_w_out = reduce_scatter_dp(scale * part_out, groups)
    grad_latents = lax.dot_general(
        table, returned, (((0,), (0,)), ((), ())), preferred_element_type=jnp.float32
    )
    grad_latents = grad_latents.astype(jnp.bfloat16)
    return (grad_latents, grad_w_in[None], grad_w_out[None])


def solution(mesh):
    return jax.shard_map(
        per_device,
        mesh=mesh,
        in_specs=(
            P(("dp", "expert"), None),
            P(("dp", "expert"), None),
            P(("dp", "expert")),
            P("expert", None, None),
            P("expert", None, None),
        ),
        out_specs=(P(("dp", "expert"), None), P("expert", "dp", None), P("expert", "dp", None)),
        check_vma=False,
    )
```

```python
import math

import jax
import jax.numpy as jnp
from jax import lax
from jax.sharding import PartitionSpec as P


def gelu_parts(value):
    coeff = 0.7978845608028654
    cube = value * value * value
    inner = jnp.tanh(coeff * (value + 0.044715 * cube))
    result = 0.5 * value * (1.0 + inner)
    slope = 0.5 * (1.0 + inner) + 0.5 * value * (1.0 - inner * inner) * coeff * (
        1.0 + 3.0 * 0.044715 * value * value
    )
    return (result, slope)


def block_pass(block, w_first, w_second):
    width = block.shape[1] // 2
    inputs = block[:, :width]
    grads = block[:, width:]
    pre_act = jnp.dot(inputs, w_first, preferred_element_type=jnp.float32)
    value, slope = gelu_parts(pre_act)
    act = value.astype(jnp.bfloat16)
    act_grad = lax.dot_general(
        grads, w_second, (((1,), (1,)), ((), ())), preferred_element_type=jnp.float32
    )
    hidden_grad = (act_grad * slope).astype(jnp.bfloat16)
    row_grad = lax.dot_general(
        hidden_grad, w_first, (((1,), (1,)), ((), ())), preferred_element_type=jnp.float32
    ).astype(jnp.bfloat16)
    return row_grad, act, hidden_grad


def weight_parts(blocks, acts, hidden_grads):
    width = blocks[0].shape[1] // 2
    block = jnp.concatenate(blocks, axis=0)
    act = jnp.concatenate(acts, axis=0)
    hidden_grad = jnp.concatenate(hidden_grads, axis=0)
    part_in = lax.dot_general(
        block[:, :width], hidden_grad, (((0,), (0,)), ((), ())),
        preferred_element_type=jnp.float32,
    )
    part_out = lax.dot_general(
        act, block[:, width:], (((0,), (0,)), ((), ())), preferred_element_type=jnp.float32
    )
    return part_in, part_out


def halve_dp(blocks, level, groups):
    axis = blocks.ndim - 3
    bit = (lax.axis_index("dp") >> level) & 1
    keep = lax.dynamic_index_in_dim(blocks, bit, axis, keepdims=False)
    send = lax.dynamic_index_in_dim(blocks, 1 - bit, axis, keepdims=False)
    got = lax.ppermute(
        send.astype(jnp.bfloat16), "dp", [(j, j ^ (1 << level)) for j in range(groups)]
    )
    return keep, got


def per_device(latents, cotangent, expert_of_row, w_in, w_out):
    rows, width = latents.shape
    experts = lax.axis_size("expert")
    groups = lax.axis_size("dp")
    capacity = 3 * rows // (2 * experts)
    slots = experts * capacity
    member = (expert_of_row[:, None] == jnp.arange(experts, dtype=jnp.int32)[None, :]).astype(
        jnp.int32
    )
    before = jnp.cumsum(member, axis=0, dtype=jnp.int32) - member
    rank = jnp.sum(before * member, axis=1, dtype=jnp.int32)
    slot = expert_of_row * capacity + rank
    stacked = jnp.concatenate([latents, cotangent], axis=1)
    table = (slot[None, :] == jnp.arange(slots, dtype=jnp.int32)[:, None]).astype(jnp.bfloat16)
    outgoing = jnp.dot(table, stacked, preferred_element_type=jnp.float32).astype(jnp.bfloat16)
    outgoing = outgoing.reshape(experts, capacity, 2 * width)
    w_first = w_in[0]
    w_second = w_out[0]

    incoming = lax.all_to_all(outgoing, "expert", 0, 0, tiled=True).reshape(slots, 2 * width)
    row_grad, act, hidden_grad = block_pass(incoming, w_first, w_second)
    scale = 1.0 / math.sqrt(groups * rows)
    part_in, part_out = weight_parts([incoming], [act], [hidden_grad])

    levels = groups.bit_length() - 1
    sums = []
    for part in (part_out, part_in):
        blocks = (scale * part).reshape((2,) * levels + (part.shape[0] // groups,) + part.shape[1:])
        for level in range(levels - 1):
            keep, got = halve_dp(blocks, level, groups)
            blocks = keep + got.astype(jnp.float32)
        sums.append(blocks)
    row_grad, sums[0], sums[1] = lax.optimization_barrier((row_grad, sums[0], sums[1]))
    finals = []
    for blocks in sums:
        keep, got = halve_dp(blocks, levels - 1, groups)
        finals.append((keep, got))
    returned = lax.all_to_all(
        row_grad.reshape(experts, capacity, width), "expert", 0, 0, tiled=True
    ).reshape(slots, width)
    grad_w_out, grad_w_in = [keep + got.astype(jnp.float32) for keep, got in finals]

    grad_latents = lax.dot_general(
        table, returned, (((0,), (0,)), ((), ())), preferred_element_type=jnp.float32
    )
    grad_latents = grad_latents.astype(jnp.bfloat16)
    return (grad_latents, grad_w_in[None], grad_w_out[None])


def solution(mesh):
    return jax.shard_map(
        per_device,
        mesh=mesh,
        in_specs=(
            P(("dp", "expert"), None),
            P(("dp", "expert"), None),
            P(("dp", "expert")),
            P("expert", None, None),
            P("expert", None, None),
        ),
        out_specs=(P(("dp", "expert"), None), P("expert", "dp", None), P("expert", "dp", None)),
        check_vma=False,
    )
```

```python
import math

import jax
import jax.numpy as jnp
from jax import lax
from jax.sharding import PartitionSpec as P


def gelu_parts(value):
    coeff = 0.7978845608028654
    cube = value * value * value
    inner = jnp.tanh(coeff * (value + 0.044715 * cube))
    result = 0.5 * value * (1.0 + inner)
    slope = 0.5 * (1.0 + inner) + 0.5 * value * (1.0 - inner * inner) * coeff * (
        1.0 + 3.0 * 0.044715 * value * value
    )
    return (result, slope)


def block_pass(block, w_first, w_second):
    width = block.shape[1] // 2
    inputs = block[:, :width]
    grads = block[:, width:]
    pre_act = jnp.dot(inputs, w_first, preferred_element_type=jnp.float32)
    value, slope = gelu_parts(pre_act)
    act = value.astype(jnp.bfloat16)
    act_grad = lax.dot_general(
        grads, w_second, (((1,), (1,)), ((), ())), preferred_element_type=jnp.float32
    )
    hidden_grad = (act_grad * slope).astype(jnp.bfloat16)
    row_grad = lax.dot_general(
        hidden_grad, w_first, (((1,), (1,)), ((), ())), preferred_element_type=jnp.float32
    ).astype(jnp.bfloat16)
    return row_grad, act, hidden_grad


def weight_parts(blocks, acts, hidden_grads):
    width = blocks[0].shape[1] // 2
    block = jnp.concatenate(blocks, axis=0)
    act = jnp.concatenate(acts, axis=0)
    hidden_grad = jnp.concatenate(hidden_grads, axis=0)
    part_in = lax.dot_general(
        block[:, :width], hidden_grad, (((0,), (0,)), ((), ())),
        preferred_element_type=jnp.float32,
    )
    part_out = lax.dot_general(
        act, block[:, width:], (((0,), (0,)), ((), ())), preferred_element_type=jnp.float32
    )
    return part_in, part_out


def halve_dp(blocks, level, groups):
    axis = blocks.ndim - 3
    bit = (lax.axis_index("dp") >> level) & 1
    keep = lax.dynamic_index_in_dim(blocks, bit, axis, keepdims=False)
    send = lax.dynamic_index_in_dim(blocks, 1 - bit, axis, keepdims=False)
    got = lax.ppermute(
        send.astype(jnp.bfloat16), "dp", [(j, j ^ (1 << level)) for j in range(groups)]
    )
    return keep, got


def per_device(latents, cotangent, expert_of_row, w_in, w_out):
    rows, width = latents.shape
    experts = lax.axis_size("expert")
    groups = lax.axis_size("dp")
    capacity = 3 * rows // (2 * experts)
    slots = experts * capacity
    member = (expert_of_row[:, None] == jnp.arange(experts, dtype=jnp.int32)[None, :]).astype(
        jnp.int32
    )
    before = jnp.cumsum(member, axis=0, dtype=jnp.int32) - member
    rank = jnp.sum(before * member, axis=1, dtype=jnp.int32)
    slot = expert_of_row * capacity + rank
    stacked = jnp.concatenate([latents, cotangent], axis=1)
    table = (slot[None, :] == jnp.arange(slots, dtype=jnp.int32)[:, None]).astype(jnp.bfloat16)
    outgoing = jnp.dot(table, stacked, preferred_element_type=jnp.float32).astype(jnp.bfloat16)
    outgoing = outgoing.reshape(experts, capacity, 2 * width)
    w_first = w_in[0]
    w_second = w_out[0]

    first = capacity // 2
    sizes = (first, capacity - first)
    sending = [outgoing[:, :first], outgoing[:, first:]]
    incoming = [lax.all_to_all(sending[0], "expert", 0, 0, tiled=True)]
    sending[1], incoming[0] = lax.optimization_barrier((sending[1], incoming[0]))
    incoming.append(lax.all_to_all(sending[1], "expert", 0, 0, tiled=True))
    scale = 1.0 / math.sqrt(groups * rows)
    row_grads = []
    part_in = part_out = None
    for half in range(2):
        block = incoming[half].reshape(experts * sizes[half], 2 * width)
        row_grad, act, hidden_grad = block_pass(block, w_first, w_second)
        if half == 0:
            incoming[1], row_grad = lax.optimization_barrier((incoming[1], row_grad))
        row_grads.append(row_grad)
        p_in, p_out = weight_parts([block], [act], [hidden_grad])
        part_in = p_in if part_in is None else part_in + p_in
        part_out = p_out if part_out is None else part_out + p_out
    back = [
        lax.all_to_all(
            row_grads[0].reshape(experts, sizes[0], width), "expert", 0, 0, tiled=True
        )
    ]
    back[0], row_grad = lax.optimization_barrier((back[0], row_grads[1]))

    levels = groups.bit_length() - 1
    sums = []
    for part in (part_out, part_in):
        blocks = (scale * part).reshape((2,) * levels + (part.shape[0] // groups,) + part.shape[1:])
        for level in range(levels - 1):
            keep, got = halve_dp(blocks, level, groups)
            blocks = keep + got.astype(jnp.float32)
        sums.append(blocks)
    row_grad, sums[0], sums[1] = lax.optimization_barrier((row_grad, sums[0], sums[1]))
    finals = []
    for blocks in sums:
        keep, got = halve_dp(blocks, levels - 1, groups)
        finals.append((keep, got))
    back.append(
        lax.all_to_all(row_grad.reshape(experts, sizes[1], width), "expert", 0, 0, tiled=True)
    )
    returned = jnp.concatenate(back, axis=1).reshape(slots, width)
    grad_w_out, grad_w_in = [keep + got.astype(jnp.float32) for keep, got in finals]

    grad_latents = lax.dot_general(
        table, returned, (((0,), (0,)), ((), ())), preferred_element_type=jnp.float32
    )
    grad_latents = grad_latents.astype(jnp.bfloat16)
    return (grad_latents, grad_w_in[None], grad_w_out[None])


def solution(mesh):
    return jax.shard_map(
        per_device,
        mesh=mesh,
        in_specs=(
            P(("dp", "expert"), None),
            P(("dp", "expert"), None),
            P(("dp", "expert")),
            P("expert", None, None),
            P("expert", None, None),
        ),
        out_specs=(P(("dp", "expert"), None), P("expert", "dp", None), P("expert", "dp", None)),
        check_vma=False,
    )
```

```python
import math

import jax
import jax.numpy as jnp
from jax import lax
from jax.sharding import PartitionSpec as P


def gelu_parts(value):
    coeff = 0.7978845608028654
    cube = value * value * value
    inner = jnp.tanh(coeff * (value + 0.044715 * cube))
    result = 0.5 * value * (1.0 + inner)
    slope = 0.5 * (1.0 + inner) + 0.5 * value * (1.0 - inner * inner) * coeff * (
        1.0 + 3.0 * 0.044715 * value * value
    )
    return (result, slope)


def hidden_pass(block, w_first, w_second):
    width = block.shape[1] // 2
    inputs = block[:, :width]
    grads = block[:, width:]
    pre_act = jnp.dot(inputs, w_first, preferred_element_type=jnp.float32)
    value, slope = gelu_parts(pre_act)
    act = value.astype(jnp.bfloat16)
    act_grad = lax.dot_general(
        grads, w_second, (((1,), (1,)), ((), ())), preferred_element_type=jnp.float32
    )
    hidden_grad = (act_grad * slope).astype(jnp.bfloat16)
    return act, hidden_grad


def row_pass(hidden_grad, w_first):
    return lax.dot_general(
        hidden_grad, w_first, (((1,), (1,)), ((), ())), preferred_element_type=jnp.float32
    ).astype(jnp.bfloat16)


def weight_parts(blocks, acts, hidden_grads):
    width = blocks[0].shape[1] // 2
    block = jnp.concatenate(blocks, axis=0)
    act = jnp.concatenate(acts, axis=0)
    hidden_grad = jnp.concatenate(hidden_grads, axis=0)
    part_in = lax.dot_general(
        block[:, :width], hidden_grad, (((0,), (0,)), ((), ())),
        preferred_element_type=jnp.float32,
    )
    part_out = lax.dot_general(
        act, block[:, width:], (((0,), (0,)), ((), ())), preferred_element_type=jnp.float32
    )
    return part_in, part_out


def halve_dp(blocks, level, groups):
    axis = blocks.ndim - 3
    bit = (lax.axis_index("dp") >> level) & 1
    keep = lax.dynamic_index_in_dim(blocks, bit, axis, keepdims=False)
    send = lax.dynamic_index_in_dim(blocks, 1 - bit, axis, keepdims=False)
    got = lax.ppermute(
        send.astype(jnp.bfloat16), "dp", [(j, j ^ (1 << level)) for j in range(groups)]
    )
    return keep, got


def per_device(latents, cotangent, expert_of_row, w_in, w_out):
    rows, width = latents.shape
    experts = lax.axis_size("expert")
    groups = lax.axis_size("dp")
    capacity = 3 * rows // (2 * experts)
    slots = experts * capacity
    member = (expert_of_row[:, None] == jnp.arange(experts, dtype=jnp.int32)[None, :]).astype(
        jnp.int32
    )
    before = jnp.cumsum(member, axis=0, dtype=jnp.int32) - member
    rank = jnp.sum(before * member, axis=1, dtype=jnp.int32)
    slot = expert_of_row * capacity + rank
    stacked = jnp.concatenate([latents, cotangent], axis=1)
    table = (slot[None, :] == jnp.arange(slots, dtype=jnp.int32)[:, None]).astype(jnp.bfloat16)
    outgoing = jnp.dot(table, stacked, preferred_element_type=jnp.float32).astype(jnp.bfloat16)
    outgoing = outgoing.reshape(experts, capacity, 2 * width)
    w_first = w_in[0]
    w_second = w_out[0]

    first = capacity // 2
    sizes = (first, capacity - first)
    sending = [outgoing[:, :first], outgoing[:, first:]]
    incoming = [lax.all_to_all(sending[0], "expert", 0, 0, tiled=True)]
    sending[1], incoming[0] = lax.optimization_barrier((sending[1], incoming[0]))
    incoming.append(lax.all_to_all(sending[1], "expert", 0, 0, tiled=True))
    scale = 1.0 / math.sqrt(groups * rows)
    levels = groups.bit_length() - 1
    blocks = [incoming[half].reshape(experts * sizes[half], 2 * width) for half in range(2)]
    act, hidden_grad = hidden_pass(blocks[0], w_first, w_second)
    row_grad = row_pass(hidden_grad, w_first)
    incoming_b, row_grad = lax.optimization_barrier((blocks[1], row_grad))
    part_in, part_out = weight_parts([blocks[0]], [act], [hidden_grad])
    back = [lax.all_to_all(row_grad.reshape(experts, sizes[0], width), "expert", 0, 0, tiled=True)]
    act, hidden_grad = hidden_pass(incoming_b, w_first, w_second)
    p_in, p_out = weight_parts([incoming_b], [act], [hidden_grad])
    part_in = part_in + p_in
    part_out = part_out + p_out

    sums = []
    for part in (part_out, part_in):
        chunked = (scale * part).reshape((2,) * levels + (part.shape[0] // groups,) + part.shape[1:])
        for level in range(levels - 1):
            keep, got = halve_dp(chunked, level, groups)
            chunked = keep + got.astype(jnp.float32)
        sums.append(chunked)
    hidden_grad, sums[0], sums[1] = lax.optimization_barrier((hidden_grad, sums[0], sums[1]))
    finals = [halve_dp(chunked, levels - 1, groups) for chunked in sums]
    row_grad = row_pass(hidden_grad, w_first)
    back[0], row_grad = lax.optimization_barrier((back[0], row_grad))
    back.append(
        lax.all_to_all(row_grad.reshape(experts, sizes[1], width), "expert", 0, 0, tiled=True)
    )
    returned = jnp.concatenate(back, axis=1).reshape(slots, width)
    grad_w_out, grad_w_in = [keep + got.astype(jnp.float32) for keep, got in finals]

    grad_latents = lax.dot_general(
        table, returned, (((0,), (0,)), ((), ())), preferred_element_type=jnp.float32
    )
    grad_latents = grad_latents.astype(jnp.bfloat16)
    return (grad_latents, grad_w_in[None], grad_w_out[None])


def solution(mesh):
    return jax.shard_map(
        per_device,
        mesh=mesh,
        in_specs=(
            P(("dp", "expert"), None),
            P(("dp", "expert"), None),
            P(("dp", "expert")),
            P("expert", None, None),
            P("expert", None, None),
        ),
        out_specs=(P(("dp", "expert"), None), P("expert", "dp", None), P("expert", "dp", None)),
        check_vma=False,
    )
```

```python
import math

import jax
import jax.numpy as jnp
from jax import lax
from jax.sharding import PartitionSpec as P


def gelu_parts(value):
    coeff = 0.7978845608028654
    cube = value * value * value
    inner = jnp.tanh(coeff * (value + 0.044715 * cube))
    result = 0.5 * value * (1.0 + inner)
    slope = 0.5 * (1.0 + inner) + 0.5 * value * (1.0 - inner * inner) * coeff * (
        1.0 + 3.0 * 0.044715 * value * value
    )
    return (result, slope)


def hidden_pass(block, w_first, w_second):
    width = block.shape[1] // 2
    inputs = block[:, :width]
    grads = block[:, width:]
    pre_act = jnp.dot(inputs, w_first, preferred_element_type=jnp.float32)
    value, slope = gelu_parts(pre_act)
    act = value.astype(jnp.bfloat16)
    act_grad = lax.dot_general(
        grads, w_second, (((1,), (1,)), ((), ())), preferred_element_type=jnp.float32
    )
    hidden_grad = (act_grad * slope).astype(jnp.bfloat16)
    return act, hidden_grad


def row_pass(hidden_grad, w_first):
    return lax.dot_general(
        hidden_grad, w_first, (((1,), (1,)), ((), ())), preferred_element_type=jnp.float32
    ).astype(jnp.bfloat16)


def weight_parts(blocks, acts, hidden_grads):
    width = blocks[0].shape[1] // 2
    block = jnp.concatenate(blocks, axis=0)
    act = jnp.concatenate(acts, axis=0)
    hidden_grad = jnp.concatenate(hidden_grads, axis=0)
    part_in = lax.dot_general(
        block[:, :width], hidden_grad, (((0,), (0,)), ((), ())),
        preferred_element_type=jnp.float32,
    )
    part_out = lax.dot_general(
        act, block[:, width:], (((0,), (0,)), ((), ())), preferred_element_type=jnp.float32
    )
    return part_in, part_out


def halve_dp(blocks, level, groups):
    axis = blocks.ndim - 3
    bit = (lax.axis_index("dp") >> level) & 1
    keep = lax.dynamic_index_in_dim(blocks, bit, axis, keepdims=False)
    send = lax.dynamic_index_in_dim(blocks, 1 - bit, axis, keepdims=False)
    got = lax.ppermute(
        send.astype(jnp.bfloat16), "dp", [(j, j ^ (1 << level)) for j in range(groups)]
    )
    return keep, got


def per_device(latents, cotangent, expert_of_row, w_in, w_out):
    rows, width = latents.shape
    experts = lax.axis_size("expert")
    groups = lax.axis_size("dp")
    capacity = 3 * rows // (2 * experts)
    slots = experts * capacity
    member = (expert_of_row[:, None] == jnp.arange(experts, dtype=jnp.int32)[None, :]).astype(
        jnp.int32
    )
    before = jnp.cumsum(member, axis=0, dtype=jnp.int32) - member
    rank = jnp.sum(before * member, axis=1, dtype=jnp.int32)
    slot = expert_of_row * capacity + rank
    stacked = jnp.concatenate([latents, cotangent], axis=1)
    table = (slot[None, :] == jnp.arange(slots, dtype=jnp.int32)[:, None]).astype(jnp.bfloat16)
    outgoing = jnp.dot(table, stacked, preferred_element_type=jnp.float32).astype(jnp.bfloat16)
    outgoing = outgoing.reshape(experts, capacity, 2 * width)
    w_first = w_in[0]
    w_second = w_out[0]

    first = capacity * 3 // 4
    sizes = (first, capacity - first)
    sending = [outgoing[:, :first], outgoing[:, first:]]
    incoming = [lax.all_to_all(sending[0], "expert", 0, 0, tiled=True)]
    sending[1], incoming[0] = lax.optimization_barrier((sending[1], incoming[0]))
    incoming.append(lax.all_to_all(sending[1], "expert", 0, 0, tiled=True))
    scale = 1.0 / math.sqrt(groups * rows)
    levels = groups.bit_length() - 1
    blocks = [incoming[half].reshape(experts * sizes[half], 2 * width) for half in range(2)]
    act, hidden_grad = hidden_pass(blocks[0], w_first, w_second)
    row_grad = row_pass(hidden_grad, w_first)
    incoming_b, row_grad = lax.optimization_barrier((blocks[1], row_grad))
    part_in, part_out = weight_parts([blocks[0]], [act], [hidden_grad])
    back = [lax.all_to_all(row_grad.reshape(experts, sizes[0], width), "expert", 0, 0, tiled=True)]
    act, hidden_grad = hidden_pass(incoming_b, w_first, w_second)
    p_in, p_out = weight_parts([incoming_b], [act], [hidden_grad])
    part_in = part_in + p_in
    part_out = part_out + p_out

    sums = []
    for part in (part_out, part_in):
        chunked = (scale * part).reshape((2,) * levels + (part.shape[0] // groups,) + part.shape[1:])
        for level in range(levels - 1):
            keep, got = halve_dp(chunked, level, groups)
            chunked = keep + got.astype(jnp.float32)
        sums.append(chunked)
    hidden_grad, sums[0], sums[1] = lax.optimization_barrier((hidden_grad, sums[0], sums[1]))
    finals = [halve_dp(chunked, levels - 1, groups) for chunked in sums]
    row_grad = row_pass(hidden_grad, w_first)
    back[0], row_grad = lax.optimization_barrier((back[0], row_grad))
    back.append(
        lax.all_to_all(row_grad.reshape(experts, sizes[1], width), "expert", 0, 0, tiled=True)
    )
    returned = jnp.concatenate(back, axis=1).reshape(slots, width)
    grad_w_out, grad_w_in = [keep + got.astype(jnp.float32) for keep, got in finals]

    grad_latents = lax.dot_general(
        table, returned, (((0,), (0,)), ((), ())), preferred_element_type=jnp.float32
    )
    grad_latents = grad_latents.astype(jnp.bfloat16)
    return (grad_latents, grad_w_in[None], grad_w_out[None])


def solution(mesh):
    return jax.shard_map(
        per_device,
        mesh=mesh,
        in_specs=(
            P(("dp", "expert"), None),
            P(("dp", "expert"), None),
            P(("dp", "expert")),
            P("expert", None, None),
            P("expert", None, None),
        ),
        out_specs=(P(("dp", "expert"), None), P("expert", "dp", None), P("expert", "dp", None)),
        check_vma=False,
    )
```

```python
import math

import jax
import jax.numpy as jnp
from jax import lax
from jax.sharding import PartitionSpec as P


def gelu_parts(value):
    coeff = 0.7978845608028654
    cube = value * value * value
    inner = jnp.tanh(coeff * (value + 0.044715 * cube))
    result = 0.5 * value * (1.0 + inner)
    slope = 0.5 * (1.0 + inner) + 0.5 * value * (1.0 - inner * inner) * coeff * (
        1.0 + 3.0 * 0.044715 * value * value
    )
    return (result, slope)


def hidden_pass(block, w_first, w_second):
    width = block.shape[1] // 2
    inputs = block[:, :width]
    grads = block[:, width:]
    pre_act = jnp.dot(inputs, w_first, preferred_element_type=jnp.float32)
    value, slope = gelu_parts(pre_act)
    act = value.astype(jnp.bfloat16)
    act_grad = lax.dot_general(
        grads, w_second, (((1,), (1,)), ((), ())), preferred_element_type=jnp.float32
    )
    hidden_grad = (act_grad * slope).astype(jnp.bfloat16)
    return act, hidden_grad


def row_pass(hidden_grad, w_first):
    return lax.dot_general(
        hidden_grad, w_first, (((1,), (1,)), ((), ())), preferred_element_type=jnp.float32
    ).astype(jnp.bfloat16)


def weight_parts(blocks, acts, hidden_grads):
    width = blocks[0].shape[1] // 2
    block = jnp.concatenate(blocks, axis=0)
    act = jnp.concatenate(acts, axis=0)
    hidden_grad = jnp.concatenate(hidden_grads, axis=0)
    part_in = lax.dot_general(
        block[:, :width], hidden_grad, (((0,), (0,)), ((), ())),
        preferred_element_type=jnp.float32,
    )
    part_out = lax.dot_general(
        act, block[:, width:], (((0,), (0,)), ((), ())), preferred_element_type=jnp.float32
    )
    return part_in, part_out


def halve_dp(blocks, level, groups):
    axis = blocks.ndim - 3
    bit = (lax.axis_index("dp") >> level) & 1
    keep = lax.dynamic_index_in_dim(blocks, bit, axis, keepdims=False)
    send = lax.dynamic_index_in_dim(blocks, 1 - bit, axis, keepdims=False)
    got = lax.ppermute(
        send.astype(jnp.bfloat16), "dp", [(j, j ^ (1 << level)) for j in range(groups)]
    )
    return keep, got


def per_device(latents, cotangent, expert_of_row, w_in, w_out):
    rows, width = latents.shape
    experts = lax.axis_size("expert")
    groups = lax.axis_size("dp")
    capacity = 3 * rows // (2 * experts)
    slots = experts * capacity
    member = (expert_of_row[:, None] == jnp.arange(experts, dtype=jnp.int32)[None, :]).astype(
        jnp.int32
    )
    before = jnp.cumsum(member, axis=0, dtype=jnp.int32) - member
    rank = jnp.sum(before * member, axis=1, dtype=jnp.int32)
    slot = expert_of_row * capacity + rank
    stacked = jnp.concatenate([latents, cotangent], axis=1)
    table = (slot[None, :] == jnp.arange(slots, dtype=jnp.int32)[:, None]).astype(jnp.bfloat16)
    outgoing = jnp.dot(table, stacked, preferred_element_type=jnp.float32).astype(jnp.bfloat16)
    outgoing = outgoing.reshape(experts, capacity, 2 * width)
    w_first = w_in[0]
    w_second = w_out[0]

    first = capacity * 3 // 4
    sizes = (first, capacity - first)
    sending = [outgoing[:, :first], outgoing[:, first:]]
    incoming = [lax.all_to_all(sending[0], "expert", 0, 0, tiled=True)]
    sending[1], incoming[0] = lax.optimization_barrier((sending[1], incoming[0]))
    incoming.append(lax.all_to_all(sending[1], "expert", 0, 0, tiled=True))
    scale = 1.0 / math.sqrt(groups * rows)
    levels = groups.bit_length() - 1
    blocks = [incoming[half].reshape(experts * sizes[half], 2 * width) for half in range(2)]
    act, hidden_a = hidden_pass(blocks[0], w_first, w_second)
    part_in, part_out = weight_parts([blocks[0]], [act], [hidden_a])
    incoming_b, part_in, part_out = lax.optimization_barrier((blocks[1], part_in, part_out))
    act, hidden_b = hidden_pass(incoming_b, w_first, w_second)
    p_in, p_out = weight_parts([incoming_b], [act], [hidden_b])
    part_in = part_in + p_in
    part_out = part_out + p_out

    sums = []
    for part in (part_out, part_in):
        chunked = (scale * part).reshape((2,) * levels + (part.shape[0] // groups,) + part.shape[1:])
        for level in range(levels - 1):
            keep, got = halve_dp(chunked, level, groups)
            chunked = keep + got.astype(jnp.float32)
        sums.append(chunked)
    hidden_a, hidden_b, sums[0], sums[1] = lax.optimization_barrier(
        (hidden_a, hidden_b, sums[0], sums[1])
    )
    finals = [halve_dp(chunked, levels - 1, groups) for chunked in sums]
    row_grad = jnp.concatenate(
        [
            row_pass(hidden_a, w_first).reshape(experts, sizes[0], width),
            row_pass(hidden_b, w_first).reshape(experts, sizes[1], width),
        ],
        axis=1,
    )
    returned = lax.all_to_all(row_grad, "expert", 0, 0, tiled=True).reshape(slots, width)
    grad_w_out, grad_w_in = [keep + got.astype(jnp.float32) for keep, got in finals]

    grad_latents = lax.dot_general(
        table, returned, (((0,), (0,)), ((), ())), preferred_element_type=jnp.float32
    )
    grad_latents = grad_latents.astype(jnp.bfloat16)
    return (grad_latents, grad_w_in[None], grad_w_out[None])


def solution(mesh):
    return jax.shard_map(
        per_device,
        mesh=mesh,
        in_specs=(
            P(("dp", "expert"), None),
            P(("dp", "expert"), None),
            P(("dp", "expert")),
            P("expert", None, None),
            P("expert", None, None),
        ),
        out_specs=(P(("dp", "expert"), None), P("expert", "dp", None), P("expert", "dp", None)),
        check_vma=False,
    )
```

```python
import math

import jax
import jax.numpy as jnp
from jax import lax
from jax.sharding import PartitionSpec as P


def gelu_parts(value):
    coeff = 0.7978845608028654
    cube = value * value * value
    inner = jnp.tanh(coeff * (value + 0.044715 * cube))
    result = 0.5 * value * (1.0 + inner)
    slope = 0.5 * (1.0 + inner) + 0.5 * value * (1.0 - inner * inner) * coeff * (
        1.0 + 3.0 * 0.044715 * value * value
    )
    return (result, slope)


def hidden_pass(block, w_first, w_second):
    width = block.shape[1] // 2
    inputs = block[:, :width]
    grads = block[:, width:]
    pre_act = jnp.dot(inputs, w_first, preferred_element_type=jnp.float32)
    value, slope = gelu_parts(pre_act)
    act = value.astype(jnp.bfloat16)
    act_grad = lax.dot_general(
        grads, w_second, (((1,), (1,)), ((), ())), preferred_element_type=jnp.float32
    )
    hidden_grad = (act_grad * slope).astype(jnp.bfloat16)
    return act, hidden_grad


def row_pass(hidden_grad, w_first):
    return lax.dot_general(
        hidden_grad, w_first, (((1,), (1,)), ((), ())), preferred_element_type=jnp.float32
    ).astype(jnp.bfloat16)


def weight_parts(blocks, acts, hidden_grads):
    width = blocks[0].shape[1] // 2
    block = jnp.concatenate(blocks, axis=0)
    act = jnp.concatenate(acts, axis=0)
    hidden_grad = jnp.concatenate(hidden_grads, axis=0)
    part_in = lax.dot_general(
        block[:, :width], hidden_grad, (((0,), (0,)), ((), ())),
        preferred_element_type=jnp.float32,
    )
    part_out = lax.dot_general(
        act, block[:, width:], (((0,), (0,)), ((), ())), preferred_element_type=jnp.float32
    )
    return part_in, part_out


def halve_dp(blocks, level, groups):
    axis = blocks.ndim - 3
    bit = (lax.axis_index("dp") >> level) & 1
    keep = lax.dynamic_index_in_dim(blocks, bit, axis, keepdims=False)
    send = lax.dynamic_index_in_dim(blocks, 1 - bit, axis, keepdims=False)
    got = lax.ppermute(
        send.astype(jnp.bfloat16), "dp", [(j, j ^ (1 << level)) for j in range(groups)]
    )
    return keep, got


def per_device(latents, cotangent, expert_of_row, w_in, w_out):
    rows, width = latents.shape
    experts = lax.axis_size("expert")
    groups = lax.axis_size("dp")
    capacity = 3 * rows // (2 * experts)
    slots = experts * capacity
    member = (expert_of_row[:, None] == jnp.arange(experts, dtype=jnp.int32)[None, :]).astype(
        jnp.int32
    )
    before = jnp.cumsum(member, axis=0, dtype=jnp.int32) - member
    rank = jnp.sum(before * member, axis=1, dtype=jnp.int32)
    slot = expert_of_row * capacity + rank
    stacked = jnp.concatenate([latents, cotangent], axis=1)
    table = (slot[None, :] == jnp.arange(slots, dtype=jnp.int32)[:, None]).astype(jnp.bfloat16)
    outgoing = jnp.dot(table, stacked, preferred_element_type=jnp.float32).astype(jnp.bfloat16)
    outgoing = outgoing.reshape(experts, capacity, 2 * width)
    w_first = w_in[0]
    w_second = w_out[0]

    first = capacity // 2
    sizes = (first, capacity - first)
    sending = [outgoing[:, :first], outgoing[:, first:]]
    incoming = [lax.all_to_all(sending[0], "expert", 0, 0, tiled=True)]
    sending[1], incoming[0] = lax.optimization_barrier((sending[1], incoming[0]))
    incoming.append(lax.all_to_all(sending[1], "expert", 0, 0, tiled=True))
    scale = 1.0 / math.sqrt(groups * rows)
    levels = groups.bit_length() - 1
    blocks = [incoming[half].reshape(experts * sizes[half], 2 * width) for half in range(2)]
    act, hidden_grad = hidden_pass(blocks[0], w_first, w_second)
    row_grad = row_pass(hidden_grad, w_first)
    incoming_b, row_grad = lax.optimization_barrier((blocks[1], row_grad))
    part_in, part_out = weight_parts([blocks[0]], [act], [hidden_grad])
    back = [lax.all_to_all(row_grad.reshape(experts, sizes[0], width), "expert", 0, 0, tiled=True)]
    inputs_b = incoming_b[:, :width]
    grads_b = incoming_b[:, width:]
    pre_act = jnp.dot(inputs_b, w_first, preferred_element_type=jnp.float32)
    value, slope = gelu_parts(pre_act)
    act = value.astype(jnp.bfloat16)
    part_out = part_out + lax.dot_general(
        act, grads_b, (((0,), (0,)), ((), ())), preferred_element_type=jnp.float32
    )

    def halve_early(part):
        chunked = (scale * part).reshape((2,) * levels + (part.shape[0] // groups,) + part.shape[1:])
        for level in range(levels - 1):
            keep, got = halve_dp(chunked, level, groups)
            chunked = keep + got.astype(jnp.float32)
        return chunked

    sum_out = halve_early(part_out)
    grads_b, slope, sum_out = lax.optimization_barrier((grads_b, slope, sum_out))
    final_out = halve_dp(sum_out, levels - 1, groups)
    act_grad = lax.dot_general(
        grads_b, w_second, (((1,), (1,)), ((), ())), preferred_element_type=jnp.float32
    )
    hidden_grad = (act_grad * slope).astype(jnp.bfloat16)
    part_in = part_in + lax.dot_general(
        inputs_b, hidden_grad, (((0,), (0,)), ((), ())), preferred_element_type=jnp.float32
    )
    sum_in = halve_early(part_in)
    hidden_grad, sum_in = lax.optimization_barrier((hidden_grad, sum_in))
    finals = [final_out, halve_dp(sum_in, levels - 1, groups)]
    row_grad = row_pass(hidden_grad, w_first)
    back[0], row_grad = lax.optimization_barrier((back[0], row_grad))
    back.append(
        lax.all_to_all(row_grad.reshape(experts, sizes[1], width), "expert", 0, 0, tiled=True)
    )
    returned = jnp.concatenate(back, axis=1).reshape(slots, width)
    grad_w_out, grad_w_in = [keep + got.astype(jnp.float32) for keep, got in finals]

    grad_latents = lax.dot_general(
        table, returned, (((0,), (0,)), ((), ())), preferred_element_type=jnp.float32
    )
    grad_latents = grad_latents.astype(jnp.bfloat16)
    return (grad_latents, grad_w_in[None], grad_w_out[None])


def solution(mesh):
    return _sharded(mesh)


def _sharded(mesh):
    return jax.shard_map(
        per_device,
        mesh=mesh,
        in_specs=(
            P(("dp", "expert"), None),
            P(("dp", "expert"), None),
            P(("dp", "expert")),
            P("expert", None, None),
            P("expert", None, None),
        ),
        out_specs=(P(("dp", "expert"), None), P("expert", "dp", None), P("expert", "dp", None)),
        check_vma=False,
    )
```

```python
import math

import jax
import jax.numpy as jnp
from jax import lax
from jax.sharding import PartitionSpec as P


def gelu_parts(value):
    coeff = 0.7978845608028654
    cube = value * value * value
    inner = jnp.tanh(coeff * (value + 0.044715 * cube))
    result = 0.5 * value * (1.0 + inner)
    slope = 0.5 * (1.0 + inner) + 0.5 * value * (1.0 - inner * inner) * coeff * (
        1.0 + 3.0 * 0.044715 * value * value
    )
    return (result, slope)


def hidden_pass(block, w_first, w_second):
    width = block.shape[1] // 2
    inputs = block[:, :width]
    grads = block[:, width:]
    pre_act = jnp.dot(inputs, w_first, preferred_element_type=jnp.float32)
    value, slope = gelu_parts(pre_act)
    act = value.astype(jnp.bfloat16)
    act_grad = lax.dot_general(
        grads, w_second, (((1,), (1,)), ((), ())), preferred_element_type=jnp.float32
    )
    hidden_grad = (act_grad * slope).astype(jnp.bfloat16)
    return act, hidden_grad


def row_pass(hidden_grad, w_first):
    return lax.dot_general(
        hidden_grad, w_first, (((1,), (1,)), ((), ())), preferred_element_type=jnp.float32
    ).astype(jnp.bfloat16)


def weight_parts(blocks, acts, hidden_grads):
    width = blocks[0].shape[1] // 2
    block = jnp.concatenate(blocks, axis=0)
    act = jnp.concatenate(acts, axis=0)
    hidden_grad = jnp.concatenate(hidden_grads, axis=0)
    part_in = lax.dot_general(
        block[:, :width], hidden_grad, (((0,), (0,)), ((), ())),
        preferred_element_type=jnp.float32,
    )
    part_out = lax.dot_general(
        act, block[:, width:], (((0,), (0,)), ((), ())), preferred_element_type=jnp.float32
    )
    return part_in, part_out


def halve_dp(blocks, level, groups):
    axis = blocks.ndim - 3
    bit = (lax.axis_index("dp") >> level) & 1
    keep = lax.dynamic_index_in_dim(blocks, bit, axis, keepdims=False)
    send = lax.dynamic_index_in_dim(blocks, 1 - bit, axis, keepdims=False)
    got = lax.ppermute(
        send.astype(jnp.bfloat16), "dp", [(j, j ^ (1 << level)) for j in range(groups)]
    )
    return keep, got


def per_device(latents, cotangent, expert_of_row, w_in, w_out):
    rows, width = latents.shape
    experts = lax.axis_size("expert")
    groups = lax.axis_size("dp")
    capacity = 3 * rows // (2 * experts)
    slots = experts * capacity
    member = (expert_of_row[:, None] == jnp.arange(experts, dtype=jnp.int32)[None, :]).astype(
        jnp.int32
    )
    before = jnp.cumsum(member, axis=0, dtype=jnp.int32) - member
    rank = jnp.sum(before * member, axis=1, dtype=jnp.int32)
    slot = expert_of_row * capacity + rank
    stacked = jnp.concatenate([latents, cotangent], axis=1)
    table = (slot[None, :] == jnp.arange(slots, dtype=jnp.int32)[:, None]).astype(jnp.bfloat16)
    w_first = w_in[0]
    w_second = w_out[0]

    first = capacity // 2
    sizes = (first, capacity - first)
    sending = []
    for half in range(2):
        inside = (rank >= half * first) & (rank < half * first + sizes[half])
        place = jnp.where(inside, expert_of_row * sizes[half] + rank - half * first, -1)
        pick = (
            place[None, :] == jnp.arange(experts * sizes[half], dtype=jnp.int32)[:, None]
        ).astype(jnp.bfloat16)
        sending.append(
            jnp.dot(pick, stacked, preferred_element_type=jnp.float32)
            .astype(jnp.bfloat16)
            .reshape(experts, sizes[half], 2 * width)
        )
    incoming = [lax.all_to_all(sending[0], "expert", 0, 0, tiled=True)]
    sending[1], incoming[0] = lax.optimization_barrier((sending[1], incoming[0]))
    incoming.append(lax.all_to_all(sending[1], "expert", 0, 0, tiled=True))
    scale = 1.0 / math.sqrt(groups * rows)
    levels = groups.bit_length() - 1
    blocks = [incoming[half].reshape(experts * sizes[half], 2 * width) for half in range(2)]
    act, hidden_grad = hidden_pass(blocks[0], w_first, w_second)
    row_grad = row_pass(hidden_grad, w_first)
    incoming_b, row_grad = lax.optimization_barrier((blocks[1], row_grad))
    part_in, part_out = weight_parts([blocks[0]], [act], [hidden_grad])
    back = [lax.all_to_all(row_grad.reshape(experts, sizes[0], width), "expert", 0, 0, tiled=True)]
    inputs_b = incoming_b[:, :width]
    grads_b = incoming_b[:, width:]
    pre_act = jnp.dot(inputs_b, w_first, preferred_element_type=jnp.float32)
    value, slope = gelu_parts(pre_act)
    act = value.astype(jnp.bfloat16)
    part_out = part_out + lax.dot_general(
        act, grads_b, (((0,), (0,)), ((), ())), preferred_element_type=jnp.float32
    )

    def halve_early(part):
        chunked = (scale * part).reshape((2,) * levels + (part.shape[0] // groups,) + part.shape[1:])
        for level in range(levels - 1):
            keep, got = halve_dp(chunked, level, groups)
            chunked = keep + got.astype(jnp.float32)
        return chunked

    sum_out = halve_early(part_out)
    grads_b, slope, sum_out = lax.optimization_barrier((grads_b, slope, sum_out))
    final_out = halve_dp(sum_out, levels - 1, groups)
    act_grad = lax.dot_general(
        grads_b, w_second, (((1,), (1,)), ((), ())), preferred_element_type=jnp.float32
    )
    hidden_grad = (act_grad * slope).astype(jnp.bfloat16)
    part_in = part_in + lax.dot_general(
        inputs_b, hidden_grad, (((0,), (0,)), ((), ())), preferred_element_type=jnp.float32
    )
    sum_in = halve_early(part_in)
    hidden_grad, sum_in = lax.optimization_barrier((hidden_grad, sum_in))
    finals = [final_out, halve_dp(sum_in, levels - 1, groups)]
    row_grad = row_pass(hidden_grad, w_first)
    back[0], row_grad = lax.optimization_barrier((back[0], row_grad))
    back.append(
        lax.all_to_all(row_grad.reshape(experts, sizes[1], width), "expert", 0, 0, tiled=True)
    )
    returned = jnp.concatenate(back, axis=1).reshape(slots, width)
    grad_w_out, grad_w_in = [keep + got.astype(jnp.float32) for keep, got in finals]

    grad_latents = lax.dot_general(
        table, returned, (((0,), (0,)), ((), ())), preferred_element_type=jnp.float32
    )
    grad_latents = grad_latents.astype(jnp.bfloat16)
    return (grad_latents, grad_w_in[None], grad_w_out[None])


def solution(mesh):
    return _sharded(mesh)


def _sharded(mesh):
    return jax.shard_map(
        per_device,
        mesh=mesh,
        in_specs=(
            P(("dp", "expert"), None),
            P(("dp", "expert"), None),
            P(("dp", "expert")),
            P("expert", None, None),
            P("expert", None, None),
        ),
        out_specs=(P(("dp", "expert"), None), P("expert", "dp", None), P("expert", "dp", None)),
        check_vma=False,
    )
```

```python
import math

import jax
import jax.numpy as jnp
from jax import lax
from jax.sharding import PartitionSpec as P


def gelu_parts(value):
    coeff = 0.7978845608028654
    cube = value * value * value
    inner = jnp.tanh(coeff * (value + 0.044715 * cube))
    result = 0.5 * value * (1.0 + inner)
    slope = 0.5 * (1.0 + inner) + 0.5 * value * (1.0 - inner * inner) * coeff * (
        1.0 + 3.0 * 0.044715 * value * value
    )
    return (result, slope)


def hidden_pass(block, w_first, w_second):
    width = block.shape[1] // 2
    inputs = block[:, :width]
    grads = block[:, width:]
    pre_act = jnp.dot(inputs, w_first, preferred_element_type=jnp.float32)
    value, slope = gelu_parts(pre_act)
    act = value.astype(jnp.bfloat16)
    act_grad = lax.dot_general(
        grads, w_second, (((1,), (1,)), ((), ())), preferred_element_type=jnp.float32
    )
    hidden_grad = (act_grad * slope).astype(jnp.bfloat16)
    return act, hidden_grad


def row_pass(hidden_grad, w_first):
    return lax.dot_general(
        hidden_grad, w_first, (((1,), (1,)), ((), ())), preferred_element_type=jnp.float32
    ).astype(jnp.bfloat16)


def weight_parts(blocks, acts, hidden_grads):
    width = blocks[0].shape[1] // 2
    block = jnp.concatenate(blocks, axis=0)
    act = jnp.concatenate(acts, axis=0)
    hidden_grad = jnp.concatenate(hidden_grads, axis=0)
    part_in = lax.dot_general(
        block[:, :width], hidden_grad, (((0,), (0,)), ((), ())),
        preferred_element_type=jnp.float32,
    )
    part_out = lax.dot_general(
        act, block[:, width:], (((0,), (0,)), ((), ())), preferred_element_type=jnp.float32
    )
    return part_in, part_out


def halve_dp(blocks, level, groups):
    axis = blocks.ndim - 3
    bit = (lax.axis_index("dp") >> level) & 1
    keep = lax.dynamic_index_in_dim(blocks, bit, axis, keepdims=False)
    send = lax.dynamic_index_in_dim(blocks, 1 - bit, axis, keepdims=False)
    got = lax.ppermute(
        send.astype(jnp.bfloat16), "dp", [(j, j ^ (1 << level)) for j in range(groups)]
    )
    return keep, got


def per_device(latents, cotangent, expert_of_row, w_in, w_out):
    rows, width = latents.shape
    experts = lax.axis_size("expert")
    groups = lax.axis_size("dp")
    capacity = 3 * rows // (2 * experts)
    slots = experts * capacity
    member = (expert_of_row[:, None] == jnp.arange(experts, dtype=jnp.int32)[None, :]).astype(
        jnp.float32
    )
    earlier = (
        jnp.arange(rows, dtype=jnp.int32)[:, None] > jnp.arange(rows, dtype=jnp.int32)[None, :]
    ).astype(jnp.float32)
    before = jnp.dot(earlier, member, preferred_element_type=jnp.float32)
    rank = jnp.sum(before * member, axis=1).astype(jnp.int32)
    first = capacity // 2
    sizes = (first, capacity - first)
    upper = (rank >= first).astype(jnp.int32)
    slot = (
        upper * (experts * first)
        + expert_of_row * jnp.where(upper == 1, sizes[1], sizes[0])
        + rank
        - upper * first
    )
    stacked = jnp.concatenate([latents, cotangent], axis=1)
    table = (slot[None, :] == jnp.arange(slots, dtype=jnp.int32)[:, None]).astype(jnp.bfloat16)
    outgoing = jnp.dot(table, stacked, preferred_element_type=jnp.float32).astype(jnp.bfloat16)
    w_first = w_in[0]
    w_second = w_out[0]

    sending = [
        outgoing[: experts * first].reshape(experts, first, 2 * width),
        outgoing[experts * first:].reshape(experts, sizes[1], 2 * width),
    ]
    incoming = [lax.all_to_all(sending[0], "expert", 0, 0, tiled=True)]
    sending[1], incoming[0] = lax.optimization_barrier((sending[1], incoming[0]))
    incoming.append(lax.all_to_all(sending[1], "expert", 0, 0, tiled=True))
    scale = 1.0 / math.sqrt(groups * rows)
    levels = groups.bit_length() - 1
    blocks = [incoming[half].reshape(experts * sizes[half], 2 * width) for half in range(2)]
    act, hidden_grad = hidden_pass(blocks[0], w_first, w_second)
    row_grad = row_pass(hidden_grad, w_first)
    incoming_b, row_grad = lax.optimization_barrier((blocks[1], row_grad))
    part_in, part_out = weight_parts([blocks[0]], [act], [hidden_grad])
    back = [lax.all_to_all(row_grad.reshape(experts, sizes[0], width), "expert", 0, 0, tiled=True)]
    act, hidden_grad = hidden_pass(incoming_b, w_first, w_second)
    p_in, p_out = weight_parts([incoming_b], [act], [hidden_grad])
    part_in = part_in + p_in
    part_out = part_out + p_out

    sums = []
    for part in (part_out, part_in):
        chunked = (scale * part).reshape((2,) * levels + (part.shape[0] // groups,) + part.shape[1:])
        for level in range(levels - 1):
            keep, got = halve_dp(chunked, level, groups)
            chunked = keep + got.astype(jnp.float32)
        sums.append(chunked)
    hidden_grad, sums[0], sums[1] = lax.optimization_barrier((hidden_grad, sums[0], sums[1]))
    finals = [halve_dp(chunked, levels - 1, groups) for chunked in sums]
    row_grad = row_pass(hidden_grad, w_first)
    back[0], row_grad = lax.optimization_barrier((back[0], row_grad))
    back.append(
        lax.all_to_all(row_grad.reshape(experts, sizes[1], width), "expert", 0, 0, tiled=True)
    )
    returned = jnp.concatenate(
        [back[0].reshape(experts * sizes[0], width), back[1].reshape(experts * sizes[1], width)],
        axis=0,
    )
    grad_w_out, grad_w_in = [keep + got.astype(jnp.float32) for keep, got in finals]

    grad_latents = lax.dot_general(
        table, returned, (((0,), (0,)), ((), ())), preferred_element_type=jnp.float32
    )
    grad_latents = grad_latents.astype(jnp.bfloat16)
    return (grad_latents, grad_w_in[None], grad_w_out[None])


def solution(mesh):
    return jax.shard_map(
        per_device,
        mesh=mesh,
        in_specs=(
            P(("dp", "expert"), None),
            P(("dp", "expert"), None),
            P(("dp", "expert")),
            P("expert", None, None),
            P("expert", None, None),
        ),
        out_specs=(P(("dp", "expert"), None), P("expert", "dp", None), P("expert", "dp", None)),
        check_vma=False,
    )
```

```python
import math

import jax
import jax.numpy as jnp
from jax import lax
from jax.sharding import PartitionSpec as P


def gelu_parts(value):
    coeff = 0.7978845608028654
    cube = value * value * value
    inner = jnp.tanh(coeff * (value + 0.044715 * cube))
    result = 0.5 * value * (1.0 + inner)
    slope = 0.5 * (1.0 + inner) + 0.5 * value * (1.0 - inner * inner) * coeff * (
        1.0 + 3.0 * 0.044715 * value * value
    )
    return (result, slope)


def hidden_pass(block, w_first, w_second):
    width = block.shape[1] // 2
    inputs = block[:, :width]
    grads = block[:, width:]
    pre_act = jnp.dot(inputs, w_first, preferred_element_type=jnp.float32)
    value, slope = gelu_parts(pre_act)
    act = value.astype(jnp.bfloat16)
    act_grad = lax.dot_general(
        grads, w_second, (((1,), (1,)), ((), ())), preferred_element_type=jnp.float32
    )
    hidden_grad = (act_grad * slope).astype(jnp.bfloat16)
    return act, hidden_grad


def row_pass(hidden_grad, w_first):
    return lax.dot_general(
        hidden_grad, w_first, (((1,), (1,)), ((), ())), preferred_element_type=jnp.float32
    ).astype(jnp.bfloat16)


def weight_parts(blocks, acts, hidden_grads):
    width = blocks[0].shape[1] // 2
    block = jnp.concatenate(blocks, axis=0)
    act = jnp.concatenate(acts, axis=0)
    hidden_grad = jnp.concatenate(hidden_grads, axis=0)
    part_in = lax.dot_general(
        block[:, :width], hidden_grad, (((0,), (0,)), ((), ())),
        preferred_element_type=jnp.float32,
    )
    part_out = lax.dot_general(
        act, block[:, width:], (((0,), (0,)), ((), ())), preferred_element_type=jnp.float32
    )
    return part_in, part_out


def halve_dp(blocks, level, groups):
    axis = blocks.ndim - 3
    bit = (lax.axis_index("dp") >> level) & 1
    keep = lax.dynamic_index_in_dim(blocks, bit, axis, keepdims=False)
    send = lax.dynamic_index_in_dim(blocks, 1 - bit, axis, keepdims=False)
    got = lax.ppermute(
        send.astype(jnp.bfloat16), "dp", [(j, j ^ (1 << level)) for j in range(groups)]
    )
    return keep, got


def per_device(latents, cotangent, expert_of_row, w_in, w_out):
    rows, width = latents.shape
    experts = lax.axis_size("expert")
    groups = lax.axis_size("dp")
    capacity = 3 * rows // (2 * experts)
    slots = experts * capacity
    member = (expert_of_row[:, None] == jnp.arange(experts, dtype=jnp.int32)[None, :]).astype(
        jnp.float32
    )
    earlier = (
        jnp.arange(rows, dtype=jnp.int32)[:, None] > jnp.arange(rows, dtype=jnp.int32)[None, :]
    ).astype(jnp.float32)
    before = jnp.dot(earlier, member, preferred_element_type=jnp.float32)
    rank = jnp.sum(before * member, axis=1).astype(jnp.int32)
    first = capacity // 2
    sizes = (first, capacity - first)
    upper = (rank >= first).astype(jnp.int32)
    slot = (
        upper * (experts * first)
        + expert_of_row * jnp.where(upper == 1, sizes[1], sizes[0])
        + rank
        - upper * first
    )
    stacked = jnp.concatenate([latents, cotangent], axis=1)
    table = (slot[None, :] == jnp.arange(slots, dtype=jnp.int32)[:, None]).astype(jnp.bfloat16)
    w_first = w_in[0]
    w_second = w_out[0]

    sending = []
    for half in range(2):
        offset = half * experts * first
        pick = (
            slot[None, :]
            == offset + jnp.arange(experts * sizes[half], dtype=jnp.int32)[:, None]
        ).astype(jnp.bfloat16)
        sending.append(
            jnp.dot(pick, stacked, preferred_element_type=jnp.float32)
            .astype(jnp.bfloat16)
            .reshape(experts, sizes[half], 2 * width)
        )
    incoming = [lax.all_to_all(sending[0], "expert", 0, 0, tiled=True)]
    sending[1], incoming[0] = lax.optimization_barrier((sending[1], incoming[0]))
    incoming.append(lax.all_to_all(sending[1], "expert", 0, 0, tiled=True))
    scale = 1.0 / math.sqrt(groups * rows)
    levels = groups.bit_length() - 1
    blocks = [incoming[half].reshape(experts * sizes[half], 2 * width) for half in range(2)]
    act, hidden_grad = hidden_pass(blocks[0], w_first, w_second)
    row_grad = row_pass(hidden_grad, w_first)
    incoming_b, row_grad = lax.optimization_barrier((blocks[1], row_grad))
    part_in, part_out = weight_parts([blocks[0]], [act], [hidden_grad])
    back = [lax.all_to_all(row_grad.reshape(experts, sizes[0], width), "expert", 0, 0, tiled=True)]
    act, hidden_grad = hidden_pass(incoming_b, w_first, w_second)
    p_in, p_out = weight_parts([incoming_b], [act], [hidden_grad])
    part_in = part_in + p_in
    part_out = part_out + p_out

    sums = []
    for part in (part_out, part_in):
        chunked = (scale * part).reshape((2,) * levels + (part.shape[0] // groups,) + part.shape[1:])
        for level in range(levels - 1):
            keep, got = halve_dp(chunked, level, groups)
            chunked = keep + got.astype(jnp.float32)
        sums.append(chunked)
    hidden_grad, sums[0], sums[1] = lax.optimization_barrier((hidden_grad, sums[0], sums[1]))
    finals = [halve_dp(chunked, levels - 1, groups) for chunked in sums]
    row_grad = row_pass(hidden_grad, w_first)
    back[0], row_grad = lax.optimization_barrier((back[0], row_grad))
    back.append(
        lax.all_to_all(row_grad.reshape(experts, sizes[1], width), "expert", 0, 0, tiled=True)
    )
    returned = jnp.concatenate(
        [back[0].reshape(experts * sizes[0], width), back[1].reshape(experts * sizes[1], width)],
        axis=0,
    )
    grad_w_out, grad_w_in = [keep + got.astype(jnp.float32) for keep, got in finals]

    grad_latents = lax.dot_general(
        table, returned, (((0,), (0,)), ((), ())), preferred_element_type=jnp.float32
    )
    grad_latents = grad_latents.astype(jnp.bfloat16)
    return (grad_latents, grad_w_in[None], grad_w_out[None])


def solution(mesh):
    return jax.shard_map(
        per_device,
        mesh=mesh,
        in_specs=(
            P(("dp", "expert"), None),
            P(("dp", "expert"), None),
            P(("dp", "expert")),
            P("expert", None, None),
            P("expert", None, None),
        ),
        out_specs=(P(("dp", "expert"), None), P("expert", "dp", None), P("expert", "dp", None)),
        check_vma=False,
    )
```

```python
import math

import jax
import jax.numpy as jnp
from jax import lax
from jax.sharding import PartitionSpec as P


def gelu_parts(value):
    coeff = 0.7978845608028654
    cube = value * value * value
    inner = jnp.tanh(coeff * (value + 0.044715 * cube))
    result = 0.5 * value * (1.0 + inner)
    slope = 0.5 * (1.0 + inner) + 0.5 * value * (1.0 - inner * inner) * coeff * (
        1.0 + 3.0 * 0.044715 * value * value
    )
    return (result, slope)


def hidden_pass(block, w_first, w_second):
    width = block.shape[1] // 2
    inputs = block[:, :width]
    grads = block[:, width:]
    pre_act = jnp.dot(inputs, w_first, preferred_element_type=jnp.float32)
    value, slope = gelu_parts(pre_act)
    act = value.astype(jnp.bfloat16)
    act_grad = lax.dot_general(
        grads, w_second, (((1,), (1,)), ((), ())), preferred_element_type=jnp.float32
    )
    hidden_grad = (act_grad * slope).astype(jnp.bfloat16)
    return act, hidden_grad


def row_pass(hidden_grad, w_first):
    return lax.dot_general(
        hidden_grad, w_first, (((1,), (1,)), ((), ())), preferred_element_type=jnp.float32
    ).astype(jnp.bfloat16)


def weight_parts(blocks, acts, hidden_grads):
    width = blocks[0].shape[1] // 2
    block = jnp.concatenate(blocks, axis=0)
    act = jnp.concatenate(acts, axis=0)
    hidden_grad = jnp.concatenate(hidden_grads, axis=0)
    part_in = lax.dot_general(
        block[:, :width], hidden_grad, (((0,), (0,)), ((), ())),
        preferred_element_type=jnp.float32,
    )
    part_out = lax.dot_general(
        act, block[:, width:], (((0,), (0,)), ((), ())), preferred_element_type=jnp.float32
    )
    return part_in, part_out


def halve_dp(blocks, level, groups):
    axis = blocks.ndim - 3
    bit = (lax.axis_index("dp") >> level) & 1
    keep = lax.dynamic_index_in_dim(blocks, bit, axis, keepdims=False)
    send = lax.dynamic_index_in_dim(blocks, 1 - bit, axis, keepdims=False)
    got = lax.ppermute(
        send.astype(jnp.bfloat16), "dp", [(j, j ^ (1 << level)) for j in range(groups)]
    )
    return keep, got


def per_device(latents, cotangent, expert_of_row, w_in, w_out):
    rows, width = latents.shape
    experts = lax.axis_size("expert")
    groups = lax.axis_size("dp")
    capacity = 3 * rows // (2 * experts)
    slots = experts * capacity
    member = (expert_of_row[:, None] == jnp.arange(experts, dtype=jnp.int32)[None, :]).astype(
        jnp.float32
    )
    earlier = (
        jnp.arange(rows, dtype=jnp.int32)[:, None] > jnp.arange(rows, dtype=jnp.int32)[None, :]
    ).astype(jnp.float32)
    before = jnp.dot(earlier, member, preferred_element_type=jnp.float32)
    rank = jnp.sum(before * member, axis=1).astype(jnp.int32)
    first = capacity // 2
    sizes = (first, capacity - first)
    upper = (rank >= first).astype(jnp.int32)
    slot = (
        upper * (experts * first)
        + expert_of_row * jnp.where(upper == 1, sizes[1], sizes[0])
        + rank
        - upper * first
    )
    stacked = jnp.concatenate([latents, cotangent], axis=1)
    table = (slot[None, :] == jnp.arange(slots, dtype=jnp.int32)[:, None]).astype(jnp.bfloat16)
    w_first = w_in[0]
    w_second = w_out[0]

    sending = []
    for half in range(2):
        offset = half * experts * first
        pick = (
            slot[None, :]
            == offset + jnp.arange(experts * sizes[half], dtype=jnp.int32)[:, None]
        ).astype(jnp.bfloat16)
        if half == 0:
            picked = jnp.dot(pick, stacked, preferred_element_type=jnp.float32)
        else:
            picked = jnp.concatenate(
                [
                    jnp.dot(pick, latents, preferred_element_type=jnp.float32),
                    jnp.dot(pick, cotangent, preferred_element_type=jnp.float32),
                ],
                axis=1,
            )
        sending.append(picked.astype(jnp.bfloat16).reshape(experts, sizes[half], 2 * width))
    incoming = [lax.all_to_all(sending[0], "expert", 0, 0, tiled=True)]
    sending[1], incoming[0] = lax.optimization_barrier((sending[1], incoming[0]))
    incoming.append(lax.all_to_all(sending[1], "expert", 0, 0, tiled=True))
    scale = 1.0 / math.sqrt(groups * rows)
    levels = groups.bit_length() - 1
    blocks = [incoming[half].reshape(experts * sizes[half], 2 * width) for half in range(2)]
    act, hidden_grad = hidden_pass(blocks[0], w_first, w_second)
    row_grad = row_pass(hidden_grad, w_first)
    incoming_b, row_grad = lax.optimization_barrier((blocks[1], row_grad))
    part_in, part_out = weight_parts([blocks[0]], [act], [hidden_grad])
    back = [lax.all_to_all(row_grad.reshape(experts, sizes[0], width), "expert", 0, 0, tiled=True)]
    act, hidden_grad = hidden_pass(incoming_b, w_first, w_second)
    p_in, p_out = weight_parts([incoming_b], [act], [hidden_grad])
    part_in = part_in + p_in
    part_out = part_out + p_out

    sums = []
    for part in (part_out, part_in):
        chunked = (scale * part).reshape((2,) * levels + (part.shape[0] // groups,) + part.shape[1:])
        for level in range(levels - 1):
            keep, got = halve_dp(chunked, level, groups)
            chunked = keep + got.astype(jnp.float32)
        sums.append(chunked)
    hidden_grad, sums[0], sums[1] = lax.optimization_barrier((hidden_grad, sums[0], sums[1]))
    finals = [halve_dp(chunked, levels - 1, groups) for chunked in sums]
    row_grad = row_pass(hidden_grad, w_first)
    back[0], row_grad = lax.optimization_barrier((back[0], row_grad))
    back.append(
        lax.all_to_all(row_grad.reshape(experts, sizes[1], width), "expert", 0, 0, tiled=True)
    )
    returned = jnp.concatenate(
        [back[0].reshape(experts * sizes[0], width), back[1].reshape(experts * sizes[1], width)],
        axis=0,
    )
    grad_w_out, grad_w_in = [keep + got.astype(jnp.float32) for keep, got in finals]

    grad_latents = lax.dot_general(
        table, returned, (((0,), (0,)), ((), ())), preferred_element_type=jnp.float32
    )
    grad_latents = grad_latents.astype(jnp.bfloat16)
    return (grad_latents, grad_w_in[None], grad_w_out[None])


def solution(mesh):
    return jax.shard_map(
        per_device,
        mesh=mesh,
        in_specs=(
            P(("dp", "expert"), None),
            P(("dp", "expert"), None),
            P(("dp", "expert")),
            P("expert", None, None),
            P("expert", None, None),
        ),
        out_specs=(P(("dp", "expert"), None), P("expert", "dp", None), P("expert", "dp", None)),
        check_vma=False,
    )
```

```python
import math

import jax
import jax.numpy as jnp
from jax import lax
from jax.sharding import PartitionSpec as P


def gelu_parts(value):
    coeff = 0.7978845608028654
    cube = value * value * value
    inner = jnp.tanh(coeff * (value + 0.044715 * cube))
    result = 0.5 * value * (1.0 + inner)
    slope = 0.5 * (1.0 + inner) + 0.5 * value * (1.0 - inner * inner) * coeff * (
        1.0 + 3.0 * 0.044715 * value * value
    )
    return (result, slope)


def hidden_pass(block, w_first, w_second):
    width = block.shape[1] // 2
    inputs = block[:, :width]
    grads = block[:, width:]
    pre_act = jnp.dot(inputs, w_first, preferred_element_type=jnp.float32)
    value, slope = gelu_parts(pre_act)
    act = value.astype(jnp.bfloat16)
    act_grad = lax.dot_general(
        grads, w_second, (((1,), (1,)), ((), ())), preferred_element_type=jnp.float32
    )
    hidden_grad = (act_grad * slope).astype(jnp.bfloat16)
    return act, hidden_grad


def row_pass(hidden_grad, w_first):
    return lax.dot_general(
        hidden_grad, w_first, (((1,), (1,)), ((), ())), preferred_element_type=jnp.float32
    ).astype(jnp.bfloat16)


def weight_parts(blocks, acts, hidden_grads):
    width = blocks[0].shape[1] // 2
    block = jnp.concatenate(blocks, axis=0)
    act = jnp.concatenate(acts, axis=0)
    hidden_grad = jnp.concatenate(hidden_grads, axis=0)
    part_in = lax.dot_general(
        block[:, :width], hidden_grad, (((0,), (0,)), ((), ())),
        preferred_element_type=jnp.float32,
    )
    part_out = lax.dot_general(
        act, block[:, width:], (((0,), (0,)), ((), ())), preferred_element_type=jnp.float32
    )
    return part_in, part_out


def halve_dp(blocks, level, groups):
    axis = blocks.ndim - 3
    bit = (lax.axis_index("dp") >> level) & 1
    keep = lax.dynamic_index_in_dim(blocks, bit, axis, keepdims=False)
    send = lax.dynamic_index_in_dim(blocks, 1 - bit, axis, keepdims=False)
    got = lax.ppermute(
        send.astype(jnp.bfloat16), "dp", [(j, j ^ (1 << level)) for j in range(groups)]
    )
    return keep, got


def per_device(latents, cotangent, expert_of_row, w_in, w_out):
    rows, width = latents.shape
    experts = lax.axis_size("expert")
    groups = lax.axis_size("dp")
    capacity = 3 * rows // (2 * experts)
    slots = experts * capacity
    member = (expert_of_row[:, None] == jnp.arange(experts, dtype=jnp.int32)[None, :]).astype(
        jnp.float32
    )
    earlier = (
        jnp.arange(rows, dtype=jnp.int32)[:, None] > jnp.arange(rows, dtype=jnp.int32)[None, :]
    ).astype(jnp.float32)
    before = jnp.dot(earlier, member, preferred_element_type=jnp.float32)
    rank = jnp.sum(before * member, axis=1).astype(jnp.int32)
    first = capacity // 2
    sizes = (first, capacity - first)
    upper = (rank >= first).astype(jnp.int32)
    slot = (
        upper * (experts * first)
        + expert_of_row * jnp.where(upper == 1, sizes[1], sizes[0])
        + rank
        - upper * first
    )
    stacked = jnp.concatenate([latents, cotangent], axis=1)
    table = (slot[None, :] == jnp.arange(slots, dtype=jnp.int32)[:, None]).astype(jnp.bfloat16)
    w_first = w_in[0]
    w_second = w_out[0]

    sending = []
    for half in range(2):
        offset = half * experts * first
        pick = (
            slot[None, :]
            == offset + jnp.arange(experts * sizes[half], dtype=jnp.int32)[:, None]
        ).astype(jnp.bfloat16)
        if half == 0:
            picked = jnp.dot(pick, stacked, preferred_element_type=jnp.float32)
        else:
            picked = jnp.concatenate(
                [
                    jnp.dot(pick, latents, preferred_element_type=jnp.float32),
                    jnp.dot(pick, cotangent, preferred_element_type=jnp.float32),
                ],
                axis=1,
            )
        sending.append(picked.astype(jnp.bfloat16).reshape(experts, sizes[half], 2 * width))
    incoming = [lax.all_to_all(sending[0], "expert", 0, 0, tiled=True)]
    sending[1], incoming[0] = lax.optimization_barrier((sending[1], incoming[0]))
    incoming.append(lax.all_to_all(sending[1], "expert", 0, 0, tiled=True))
    scale = 1.0 / math.sqrt(groups * rows)
    levels = groups.bit_length() - 1
    blocks = [incoming[half].reshape(experts * sizes[half], 2 * width) for half in range(2)]
    act, hidden_grad = hidden_pass(blocks[0], w_first, w_second)
    row_grad = row_pass(hidden_grad, w_first)
    incoming_b, row_grad = lax.optimization_barrier((blocks[1], row_grad))
    part_in, part_out = weight_parts([blocks[0]], [act], [hidden_grad])
    back = [lax.all_to_all(row_grad.reshape(experts, sizes[0], width), "expert", 0, 0, tiled=True)]
    act, hidden_grad = hidden_pass(incoming_b, w_first, w_second)
    p_in, p_out = weight_parts([incoming_b], [act], [hidden_grad])
    part_in = part_in + p_in
    part_out = part_out + p_out

    sums = []
    for part in (part_out, part_in):
        chunked = (scale * part).reshape((2,) * levels + (part.shape[0] // groups,) + part.shape[1:])
        for level in range(levels - 1):
            keep, got = halve_dp(chunked, level, groups)
            chunked = keep + got.astype(jnp.float32)
        sums.append(chunked)
    hidden_grad, sums[0], sums[1] = lax.optimization_barrier((hidden_grad, sums[0], sums[1]))
    finals = [halve_dp(chunked, levels - 1, groups) for chunked in sums]
    row_grad = row_pass(hidden_grad, w_first)
    back[0], row_grad = lax.optimization_barrier((back[0], row_grad))
    back.append(
        lax.all_to_all(row_grad.reshape(experts, sizes[1], width), "expert", 0, 0, tiled=True)
    )
    grad_w_out, grad_w_in = [keep + got.astype(jnp.float32) for keep, got in finals]

    combined = [
        lax.dot_general(
            table[half * experts * first:half * experts * first + experts * sizes[half]],
            back[half].reshape(experts * sizes[half], width),
            (((0,), (0,)), ((), ())),
            preferred_element_type=jnp.float32,
        )
        for half in range(2)
    ]
    grad_latents = (combined[0] + combined[1]).astype(jnp.bfloat16)
    return (grad_latents, grad_w_in[None], grad_w_out[None])


def solution(mesh):
    return jax.shard_map(
        per_device,
        mesh=mesh,
        in_specs=(
            P(("dp", "expert"), None),
            P(("dp", "expert"), None),
            P(("dp", "expert")),
            P("expert", None, None),
            P("expert", None, None),
        ),
        out_specs=(P(("dp", "expert"), None), P("expert", "dp", None), P("expert", "dp", None)),
        check_vma=False,
    )
```

```python
import math

import jax
import jax.numpy as jnp
from jax import lax
from jax.sharding import PartitionSpec as P


def gelu_parts(value):
    coeff = 0.7978845608028654
    cube = value * value * value
    inner = jnp.tanh(coeff * (value + 0.044715 * cube))
    result = 0.5 * value * (1.0 + inner)
    slope = 0.5 * (1.0 + inner) + 0.5 * value * (1.0 - inner * inner) * coeff * (
        1.0 + 3.0 * 0.044715 * value * value
    )
    return (result, slope)


def hidden_pass(block, w_first, w_second):
    width = block.shape[1] // 2
    inputs = block[:, :width]
    grads = block[:, width:]
    pre_act = jnp.dot(inputs, w_first, preferred_element_type=jnp.float32)
    value, slope = gelu_parts(pre_act)
    act = value.astype(jnp.bfloat16)
    act_grad = lax.dot_general(
        grads, w_second, (((1,), (1,)), ((), ())), preferred_element_type=jnp.float32
    )
    hidden_grad = (act_grad * slope).astype(jnp.bfloat16)
    return act, hidden_grad


def row_pass(hidden_grad, w_first):
    return lax.dot_general(
        hidden_grad, w_first, (((1,), (1,)), ((), ())), preferred_element_type=jnp.float32
    ).astype(jnp.bfloat16)


def weight_parts(blocks, acts, hidden_grads):
    width = blocks[0].shape[1] // 2
    block = jnp.concatenate(blocks, axis=0)
    act = jnp.concatenate(acts, axis=0)
    hidden_grad = jnp.concatenate(hidden_grads, axis=0)
    part_in = lax.dot_general(
        block[:, :width], hidden_grad, (((0,), (0,)), ((), ())),
        preferred_element_type=jnp.float32,
    )
    part_out = lax.dot_general(
        act, block[:, width:], (((0,), (0,)), ((), ())), preferred_element_type=jnp.float32
    )
    return part_in, part_out


def halve_dp(blocks, level, groups):
    axis = blocks.ndim - 3
    bit = (lax.axis_index("dp") >> level) & 1
    keep = lax.dynamic_index_in_dim(blocks, bit, axis, keepdims=False)
    send = lax.dynamic_index_in_dim(blocks, 1 - bit, axis, keepdims=False)
    got = lax.ppermute(
        send.astype(jnp.bfloat16), "dp", [(j, j ^ (1 << level)) for j in range(groups)]
    )
    return keep, got


def per_device(latents, cotangent, expert_of_row, w_in, w_out):
    rows, width = latents.shape
    experts = lax.axis_size("expert")
    groups = lax.axis_size("dp")
    capacity = 3 * rows // (2 * experts)
    slots = experts * capacity
    member = (expert_of_row[:, None] == jnp.arange(experts, dtype=jnp.int32)[None, :]).astype(
        jnp.float32
    )
    earlier = (
        jnp.arange(rows, dtype=jnp.int32)[:, None] > jnp.arange(rows, dtype=jnp.int32)[None, :]
    ).astype(jnp.float32)
    before = jnp.dot(earlier, member, preferred_element_type=jnp.float32)
    rank = jnp.sum(before * member, axis=1).astype(jnp.int32)
    first = capacity * 7 // 12
    sizes = (first, capacity - first)
    upper = (rank >= first).astype(jnp.int32)
    slot = (
        upper * (experts * first)
        + expert_of_row * jnp.where(upper == 1, sizes[1], sizes[0])
        + rank
        - upper * first
    )
    stacked = jnp.concatenate([latents, cotangent], axis=1)
    table = (slot[None, :] == jnp.arange(slots, dtype=jnp.int32)[:, None]).astype(jnp.bfloat16)
    w_first = w_in[0]
    w_second = w_out[0]

    sending = []
    for half in range(2):
        offset = half * experts * first
        pick = (
            slot[None, :]
            == offset + jnp.arange(experts * sizes[half], dtype=jnp.int32)[:, None]
        ).astype(jnp.bfloat16)
        if half == 0:
            picked = jnp.dot(pick, stacked, preferred_element_type=jnp.float32)
        else:
            picked = jnp.concatenate(
                [
                    jnp.dot(pick, latents, preferred_element_type=jnp.float32),
                    jnp.dot(pick, cotangent, preferred_element_type=jnp.float32),
                ],
                axis=1,
            )
        sending.append(picked.astype(jnp.bfloat16).reshape(experts, sizes[half], 2 * width))
    incoming = [lax.all_to_all(sending[0], "expert", 0, 0, tiled=True)]
    sending[1], incoming[0] = lax.optimization_barrier((sending[1], incoming[0]))
    incoming.append(lax.all_to_all(sending[1], "expert", 0, 0, tiled=True))
    scale = 1.0 / math.sqrt(groups * rows)
    levels = groups.bit_length() - 1
    blocks = [incoming[half].reshape(experts * sizes[half], 2 * width) for half in range(2)]
    act, hidden_grad = hidden_pass(blocks[0], w_first, w_second)
    row_grad = row_pass(hidden_grad, w_first)
    incoming_b, row_grad = lax.optimization_barrier((blocks[1], row_grad))
    part_in, part_out = weight_parts([blocks[0]], [act], [hidden_grad])
    back = [lax.all_to_all(row_grad.reshape(experts, sizes[0], width), "expert", 0, 0, tiled=True)]
    act, hidden_grad = hidden_pass(incoming_b, w_first, w_second)
    p_in, p_out = weight_parts([incoming_b], [act], [hidden_grad])
    part_in = part_in + p_in
    part_out = part_out + p_out

    sums = []
    for part in (part_out, part_in):
        chunked = (scale * part).reshape((2,) * levels + (part.shape[0] // groups,) + part.shape[1:])
        for level in range(levels - 1):
            keep, got = halve_dp(chunked, level, groups)
            chunked = keep + got.astype(jnp.float32)
        sums.append(chunked)
    hidden_grad, sums[0], sums[1] = lax.optimization_barrier((hidden_grad, sums[0], sums[1]))
    finals = [halve_dp(chunked, levels - 1, groups) for chunked in sums]
    row_grad = row_pass(hidden_grad, w_first)
    back[0], row_grad = lax.optimization_barrier((back[0], row_grad))
    back.append(
        lax.all_to_all(row_grad.reshape(experts, sizes[1], width), "expert", 0, 0, tiled=True)
    )
    returned = jnp.concatenate(
        [back[0].reshape(experts * sizes[0], width), back[1].reshape(experts * sizes[1], width)],
        axis=0,
    )
    grad_w_out, grad_w_in = [keep + got.astype(jnp.float32) for keep, got in finals]

    grad_latents = lax.dot_general(
        table, returned, (((0,), (0,)), ((), ())), preferred_element_type=jnp.float32
    )
    grad_latents = grad_latents.astype(jnp.bfloat16)
    return (grad_latents, grad_w_in[None], grad_w_out[None])


def solution(mesh):
    return jax.shard_map(
        per_device,
        mesh=mesh,
        in_specs=(
            P(("dp", "expert"), None),
            P(("dp", "expert"), None),
            P(("dp", "expert")),
            P("expert", None, None),
            P("expert", None, None),
        ),
        out_specs=(P(("dp", "expert"), None), P("expert", "dp", None), P("expert", "dp", None)),
        check_vma=False,
    )
```

```python
import math

import jax
import jax.numpy as jnp
from jax import lax
from jax.sharding import PartitionSpec as P


def gelu_parts(value):
    coeff = 0.7978845608028654
    cube = value * value * value
    inner = jnp.tanh(coeff * (value + 0.044715 * cube))
    result = 0.5 * value * (1.0 + inner)
    slope = 0.5 * (1.0 + inner) + 0.5 * value * (1.0 - inner * inner) * coeff * (
        1.0 + 3.0 * 0.044715 * value * value
    )
    return (result, slope)


def hidden_pass(block, w_first, w_second):
    width = block.shape[1] // 2
    inputs = block[:, :width]
    grads = block[:, width:]
    pre_act = jnp.dot(inputs, w_first, preferred_element_type=jnp.float32)
    value, slope = gelu_parts(pre_act)
    act = value.astype(jnp.bfloat16)
    act_grad = lax.dot_general(
        grads, w_second, (((1,), (1,)), ((), ())), preferred_element_type=jnp.float32
    )
    hidden_grad = (act_grad * slope).astype(jnp.bfloat16)
    return act, hidden_grad


def row_pass(hidden_grad, w_first):
    return lax.dot_general(
        hidden_grad, w_first, (((1,), (1,)), ((), ())), preferred_element_type=jnp.float32
    ).astype(jnp.bfloat16)


def weight_parts(blocks, acts, hidden_grads):
    width = blocks[0].shape[1] // 2
    block = jnp.concatenate(blocks, axis=0)
    act = jnp.concatenate(acts, axis=0)
    hidden_grad = jnp.concatenate(hidden_grads, axis=0)
    part_in = lax.dot_general(
        block[:, :width], hidden_grad, (((0,), (0,)), ((), ())),
        preferred_element_type=jnp.float32,
    )
    part_out = lax.dot_general(
        act, block[:, width:], (((0,), (0,)), ((), ())), preferred_element_type=jnp.float32
    )
    return part_in, part_out


def halve_dp(blocks, level, groups):
    axis = blocks.ndim - 3
    bit = (lax.axis_index("dp") >> level) & 1
    keep = lax.dynamic_index_in_dim(blocks, bit, axis, keepdims=False)
    send = lax.dynamic_index_in_dim(blocks, 1 - bit, axis, keepdims=False)
    got = lax.ppermute(
        send.astype(jnp.bfloat16), "dp", [(j, j ^ (1 << level)) for j in range(groups)]
    )
    return keep, got


def per_device(latents, cotangent, expert_of_row, w_in, w_out):
    rows, width = latents.shape
    experts = lax.axis_size("expert")
    groups = lax.axis_size("dp")
    capacity = 3 * rows // (2 * experts)
    slots = experts * capacity
    member = (expert_of_row[:, None] == jnp.arange(experts, dtype=jnp.int32)[None, :]).astype(
        jnp.float32
    )
    earlier = (
        jnp.arange(rows, dtype=jnp.int32)[:, None] > jnp.arange(rows, dtype=jnp.int32)[None, :]
    ).astype(jnp.float32)
    before = jnp.dot(earlier, member, preferred_element_type=jnp.float32)
    rank = jnp.sum(before * member, axis=1).astype(jnp.int32)
    first = capacity * 2 // 3
    sizes = (first, capacity - first)
    upper = (rank >= first).astype(jnp.int32)
    slot = (
        upper * (experts * first)
        + expert_of_row * jnp.where(upper == 1, sizes[1], sizes[0])
        + rank
        - upper * first
    )
    stacked = jnp.concatenate([latents, cotangent], axis=1)
    table = (slot[None, :] == jnp.arange(slots, dtype=jnp.int32)[:, None]).astype(jnp.bfloat16)
    w_first = w_in[0]
    w_second = w_out[0]

    sending = []
    for half in range(2):
        offset = half * experts * first
        pick = (
            slot[None, :]
            == offset + jnp.arange(experts * sizes[half], dtype=jnp.int32)[:, None]
        ).astype(jnp.bfloat16)
        if half == 0:
            picked = jnp.dot(pick, stacked, preferred_element_type=jnp.float32)
        else:
            picked = jnp.concatenate(
                [
                    jnp.dot(pick, latents, preferred_element_type=jnp.float32),
                    jnp.dot(pick, cotangent, preferred_element_type=jnp.float32),
                ],
                axis=1,
            )
        sending.append(picked.astype(jnp.bfloat16).reshape(experts, sizes[half], 2 * width))
    incoming = [lax.all_to_all(sending[0], "expert", 0, 0, tiled=True)]
    sending[1], incoming[0] = lax.optimization_barrier((sending[1], incoming[0]))
    incoming.append(lax.all_to_all(sending[1], "expert", 0, 0, tiled=True))
    scale = 1.0 / math.sqrt(groups * rows)
    levels = groups.bit_length() - 1
    blocks = [incoming[half].reshape(experts * sizes[half], 2 * width) for half in range(2)]
    act, hidden_grad = hidden_pass(blocks[0], w_first, w_second)
    row_grad = row_pass(hidden_grad, w_first)
    incoming_b, row_grad = lax.optimization_barrier((blocks[1], row_grad))
    part_in, part_out = weight_parts([blocks[0]], [act], [hidden_grad])
    back = [lax.all_to_all(row_grad.reshape(experts, sizes[0], width), "expert", 0, 0, tiled=True)]
    act, hidden_grad = hidden_pass(incoming_b, w_first, w_second)
    p_in, p_out = weight_parts([incoming_b], [act], [hidden_grad])
    part_in = part_in + p_in
    part_out = part_out + p_out

    sums = []
    for part in (part_out, part_in):
        chunked = (scale * part).reshape((2,) * levels + (part.shape[0] // groups,) + part.shape[1:])
        for level in range(levels - 1):
            keep, got = halve_dp(chunked, level, groups)
            chunked = keep + got.astype(jnp.float32)
        sums.append(chunked)
    hidden_grad, sums[0], sums[1] = lax.optimization_barrier((hidden_grad, sums[0], sums[1]))
    finals = [halve_dp(chunked, levels - 1, groups) for chunked in sums]
    row_grad = row_pass(hidden_grad, w_first)
    back[0], row_grad = lax.optimization_barrier((back[0], row_grad))
    back.append(
        lax.all_to_all(row_grad.reshape(experts, sizes[1], width), "expert", 0, 0, tiled=True)
    )
    returned = jnp.concatenate(
        [back[0].reshape(experts * sizes[0], width), back[1].reshape(experts * sizes[1], width)],
        axis=0,
    )
    grad_w_out, grad_w_in = [keep + got.astype(jnp.float32) for keep, got in finals]

    grad_latents = lax.dot_general(
        table, returned, (((0,), (0,)), ((), ())), preferred_element_type=jnp.float32
    )
    grad_latents = grad_latents.astype(jnp.bfloat16)
    return (grad_latents, grad_w_in[None], grad_w_out[None])


def solution(mesh):
    return jax.shard_map(
        per_device,
        mesh=mesh,
        in_specs=(
            P(("dp", "expert"), None),
            P(("dp", "expert"), None),
            P(("dp", "expert")),
            P("expert", None, None),
            P("expert", None, None),
        ),
        out_specs=(P(("dp", "expert"), None), P("expert", "dp", None), P("expert", "dp", None)),
        check_vma=False,
    )
```

```python
import math

import jax
import jax.numpy as jnp
from jax import lax
from jax.sharding import PartitionSpec as P


def gelu_parts(value):
    coeff = 0.7978845608028654
    cube = value * value * value
    inner = jnp.tanh(coeff * (value + 0.044715 * cube))
    result = 0.5 * value * (1.0 + inner)
    slope = 0.5 * (1.0 + inner) + 0.5 * value * (1.0 - inner * inner) * coeff * (
        1.0 + 3.0 * 0.044715 * value * value
    )
    return (result, slope)


def hidden_pass(block, w_first, w_second):
    width = block.shape[1] // 2
    inputs = block[:, :width]
    grads = block[:, width:]
    pre_act = jnp.dot(inputs, w_first, preferred_element_type=jnp.float32)
    value, slope = gelu_parts(pre_act)
    act = value.astype(jnp.bfloat16)
    act_grad = lax.dot_general(
        grads, w_second, (((1,), (1,)), ((), ())), preferred_element_type=jnp.float32
    )
    hidden_grad = (act_grad * slope).astype(jnp.bfloat16)
    return act, hidden_grad


def row_pass(hidden_grad, w_first):
    return lax.dot_general(
        hidden_grad, w_first, (((1,), (1,)), ((), ())), preferred_element_type=jnp.float32
    ).astype(jnp.bfloat16)


def weight_parts(blocks, acts, hidden_grads):
    width = blocks[0].shape[1] // 2
    block = jnp.concatenate(blocks, axis=0)
    act = jnp.concatenate(acts, axis=0)
    hidden_grad = jnp.concatenate(hidden_grads, axis=0)
    part_in = lax.dot_general(
        block[:, :width], hidden_grad, (((0,), (0,)), ((), ())),
        preferred_element_type=jnp.float32,
    )
    part_out = lax.dot_general(
        act, block[:, width:], (((0,), (0,)), ((), ())), preferred_element_type=jnp.float32
    )
    return part_in, part_out


def halve_dp(blocks, level, groups):
    axis = blocks.ndim - 3
    bit = (lax.axis_index("dp") >> level) & 1
    keep = lax.dynamic_index_in_dim(blocks, bit, axis, keepdims=False)
    send = lax.dynamic_index_in_dim(blocks, 1 - bit, axis, keepdims=False)
    got = lax.ppermute(
        send.astype(jnp.bfloat16), "dp", [(j, j ^ (1 << level)) for j in range(groups)]
    )
    return keep, got


def per_device(latents, cotangent, expert_of_row, w_in, w_out):
    rows, width = latents.shape
    experts = lax.axis_size("expert")
    groups = lax.axis_size("dp")
    capacity = 3 * rows // (2 * experts)
    slots = experts * capacity
    member = (expert_of_row[:, None] == jnp.arange(experts, dtype=jnp.int32)[None, :]).astype(
        jnp.float32
    )
    earlier = (
        jnp.arange(rows, dtype=jnp.int32)[:, None] > jnp.arange(rows, dtype=jnp.int32)[None, :]
    ).astype(jnp.float32)
    before = jnp.dot(earlier, member, preferred_element_type=jnp.float32)
    rank = jnp.sum(before * member, axis=1).astype(jnp.int32)
    first = capacity * 5 // 8
    sizes = (first, capacity - first)
    upper = (rank >= first).astype(jnp.int32)
    slot = (
        upper * (experts * first)
        + expert_of_row * jnp.where(upper == 1, sizes[1], sizes[0])
        + rank
        - upper * first
    )
    stacked = jnp.concatenate([latents, cotangent], axis=1)
    table = (slot[None, :] == jnp.arange(slots, dtype=jnp.int32)[:, None]).astype(jnp.bfloat16)
    w_first = w_in[0]
    w_second = w_out[0]

    sending = []
    for half in range(2):
        offset = half * experts * first
        pick = (
            slot[None, :]
            == offset + jnp.arange(experts * sizes[half], dtype=jnp.int32)[:, None]
        ).astype(jnp.bfloat16)
        if half == 0:
            picked = jnp.dot(pick, stacked, preferred_element_type=jnp.float32)
        else:
            picked = jnp.concatenate(
                [
                    jnp.dot(pick, latents, preferred_element_type=jnp.float32),
                    jnp.dot(pick, cotangent, preferred_element_type=jnp.float32),
                ],
                axis=1,
            )
        sending.append(picked.astype(jnp.bfloat16).reshape(experts, sizes[half], 2 * width))
    incoming = [lax.all_to_all(sending[0], "expert", 0, 0, tiled=True)]
    sending[1], incoming[0] = lax.optimization_barrier((sending[1], incoming[0]))
    incoming.append(lax.all_to_all(sending[1], "expert", 0, 0, tiled=True))
    scale = 1.0 / math.sqrt(groups * rows)
    levels = groups.bit_length() - 1
    blocks = [incoming[half].reshape(experts * sizes[half], 2 * width) for half in range(2)]
    act, hidden_grad = hidden_pass(blocks[0], w_first, w_second)
    row_grad = row_pass(hidden_grad, w_first)
    incoming_b, row_grad = lax.optimization_barrier((blocks[1], row_grad))
    part_in, part_out = weight_parts([blocks[0]], [act], [hidden_grad])
    back = [lax.all_to_all(row_grad.reshape(experts, sizes[0], width), "expert", 0, 0, tiled=True)]
    act, hidden_grad = hidden_pass(incoming_b, w_first, w_second)
    p_in, p_out = weight_parts([incoming_b], [act], [hidden_grad])
    part_in = part_in + p_in
    part_out = part_out + p_out

    sums = []
    for part in (part_out, part_in):
        chunked = (scale * part).reshape((2,) * levels + (part.shape[0] // groups,) + part.shape[1:])
        for level in range(levels - 1):
            keep, got = halve_dp(chunked, level, groups)
            chunked = keep + got.astype(jnp.float32)
        sums.append(chunked)
    hidden_grad, sums[0], sums[1] = lax.optimization_barrier((hidden_grad, sums[0], sums[1]))
    finals = [halve_dp(chunked, levels - 1, groups) for chunked in sums]
    row_grad = row_pass(hidden_grad, w_first)
    back[0], row_grad = lax.optimization_barrier((back[0], row_grad))
    back.append(
        lax.all_to_all(row_grad.reshape(experts, sizes[1], width), "expert", 0, 0, tiled=True)
    )
    returned = jnp.concatenate(
        [back[0].reshape(experts * sizes[0], width), back[1].reshape(experts * sizes[1], width)],
        axis=0,
    )
    grad_w_out, grad_w_in = [keep + got.astype(jnp.float32) for keep, got in finals]

    grad_latents = lax.dot_general(
        table, returned, (((0,), (0,)), ((), ())), preferred_element_type=jnp.float32
    )
    grad_latents = grad_latents.astype(jnp.bfloat16)
    return (grad_latents, grad_w_in[None], grad_w_out[None])


def solution(mesh):
    return jax.shard_map(
        per_device,
        mesh=mesh,
        in_specs=(
            P(("dp", "expert"), None),
            P(("dp", "expert"), None),
            P(("dp", "expert")),
            P("expert", None, None),
            P("expert", None, None),
        ),
        out_specs=(P(("dp", "expert"), None), P("expert", "dp", None), P("expert", "dp", None)),
        check_vma=False,
    )
```

```python
import math

import jax
import jax.numpy as jnp
from jax import lax
from jax.sharding import PartitionSpec as P


def gelu_parts(value):
    coeff = 0.7978845608028654
    cube = value * value * value
    inner = jnp.tanh(coeff * (value + 0.044715 * cube))
    result = 0.5 * value * (1.0 + inner)
    slope = 0.5 * (1.0 + inner) + 0.5 * value * (1.0 - inner * inner) * coeff * (
        1.0 + 3.0 * 0.044715 * value * value
    )
    return (result, slope)


def hidden_pass(block, w_first, w_second):
    width = block.shape[1] // 2
    inputs = block[:, :width]
    grads = block[:, width:]
    pre_act = jnp.dot(inputs, w_first, preferred_element_type=jnp.float32)
    value, slope = gelu_parts(pre_act)
    act = value.astype(jnp.bfloat16)
    act_grad = lax.dot_general(
        grads, w_second, (((1,), (1,)), ((), ())), preferred_element_type=jnp.float32
    )
    hidden_grad = (act_grad * slope).astype(jnp.bfloat16)
    return act, hidden_grad


def row_pass(hidden_grad, w_first):
    return lax.dot_general(
        hidden_grad, w_first, (((1,), (1,)), ((), ())), preferred_element_type=jnp.float32
    ).astype(jnp.bfloat16)


def weight_parts(blocks, acts, hidden_grads):
    width = blocks[0].shape[1] // 2
    block = jnp.concatenate(blocks, axis=0)
    act = jnp.concatenate(acts, axis=0)
    hidden_grad = jnp.concatenate(hidden_grads, axis=0)
    part_in = lax.dot_general(
        block[:, :width], hidden_grad, (((0,), (0,)), ((), ())),
        preferred_element_type=jnp.float32,
    )
    part_out = lax.dot_general(
        act, block[:, width:], (((0,), (0,)), ((), ())), preferred_element_type=jnp.float32
    )
    return part_in, part_out


def halve_dp(blocks, level, groups):
    axis = blocks.ndim - 3
    bit = (lax.axis_index("dp") >> level) & 1
    keep = lax.dynamic_index_in_dim(blocks, bit, axis, keepdims=False)
    send = lax.dynamic_index_in_dim(blocks, 1 - bit, axis, keepdims=False)
    got = lax.ppermute(
        send.astype(jnp.bfloat16), "dp", [(j, j ^ (1 << level)) for j in range(groups)]
    )
    return keep, got


def per_device(latents, cotangent, expert_of_row, w_in, w_out):
    rows, width = latents.shape
    experts = lax.axis_size("expert")
    groups = lax.axis_size("dp")
    capacity = 3 * rows // (2 * experts)
    slots = experts * capacity
    member = (expert_of_row[:, None] == jnp.arange(experts, dtype=jnp.int32)[None, :]).astype(
        jnp.float32
    )
    earlier = (
        jnp.arange(rows, dtype=jnp.int32)[:, None] > jnp.arange(rows, dtype=jnp.int32)[None, :]
    ).astype(jnp.float32)
    before = jnp.dot(earlier, member, preferred_element_type=jnp.float32)
    rank = jnp.sum(before * member, axis=1).astype(jnp.int32)
    first = capacity // 2
    sizes = (first, capacity - first)
    upper = (rank >= first).astype(jnp.int32)
    slot = (
        upper * (experts * first)
        + expert_of_row * jnp.where(upper == 1, sizes[1], sizes[0])
        + rank
        - upper * first
    )
    stacked = jnp.concatenate([latents, cotangent], axis=1)
    table = (slot[None, :] == jnp.arange(slots, dtype=jnp.int32)[:, None]).astype(jnp.bfloat16)
    w_first = w_in[0]
    w_second = w_out[0]

    sending = []
    for half in range(2):
        offset = half * experts * first
        pick = (
            slot[None, :]
            == offset + jnp.arange(experts * sizes[half], dtype=jnp.int32)[:, None]
        ).astype(jnp.bfloat16)
        if half == 0:
            picked = jnp.dot(pick, stacked, preferred_element_type=jnp.float32)
        else:
            picked = jnp.concatenate(
                [
                    jnp.dot(pick, latents, preferred_element_type=jnp.float32),
                    jnp.dot(pick, cotangent, preferred_element_type=jnp.float32),
                ],
                axis=1,
            )
        sending.append(picked.astype(jnp.bfloat16).reshape(experts, sizes[half], 2 * width))
    incoming = [lax.all_to_all(sending[0], "expert", 0, 0, tiled=True)]
    sending[1], incoming[0] = lax.optimization_barrier((sending[1], incoming[0]))
    incoming.append(lax.all_to_all(sending[1], "expert", 0, 0, tiled=True))
    scale = 1.0 / math.sqrt(groups * rows)
    levels = groups.bit_length() - 1
    blocks = [incoming[half].reshape(experts * sizes[half], 2 * width) for half in range(2)]
    act, hidden_grad = hidden_pass(blocks[0], w_first, w_second)
    row_grad = row_pass(hidden_grad, w_first)
    incoming_b, row_grad = lax.optimization_barrier((blocks[1], row_grad))
    part_in, part_out = weight_parts([blocks[0]], [act], [hidden_grad])
    back = [lax.all_to_all(row_grad.reshape(experts, sizes[0], width), "expert", 0, 0, tiled=True)]
    inputs_b = incoming_b[:, :width]
    grads_b = incoming_b[:, width:]
    pre_act = jnp.dot(inputs_b, w_first, preferred_element_type=jnp.float32)
    value, slope = gelu_parts(pre_act)
    act = value.astype(jnp.bfloat16)
    part_out = part_out + lax.dot_general(
        act, grads_b, (((0,), (0,)), ((), ())), preferred_element_type=jnp.float32
    )

    def halve_early(part):
        chunked = (scale * part).reshape((2,) * levels + (part.shape[0] // groups,) + part.shape[1:])
        for level in range(levels - 1):
            keep, got = halve_dp(chunked, level, groups)
            chunked = keep + got.astype(jnp.float32)
        return chunked

    sum_out = halve_early(part_out)
    grads_b, slope, sum_out = lax.optimization_barrier((grads_b, slope, sum_out))
    final_out = halve_dp(sum_out, levels - 1, groups)
    act_grad = lax.dot_general(
        grads_b, w_second, (((1,), (1,)), ((), ())), preferred_element_type=jnp.float32
    )
    hidden_grad = (act_grad * slope).astype(jnp.bfloat16)
    part_in = part_in + lax.dot_general(
        inputs_b, hidden_grad, (((0,), (0,)), ((), ())), preferred_element_type=jnp.float32
    )
    sum_in = halve_early(part_in)
    hidden_grad, sum_in = lax.optimization_barrier((hidden_grad, sum_in))
    finals = [final_out, halve_dp(sum_in, levels - 1, groups)]
    row_grad = row_pass(hidden_grad, w_first)
    back[0], row_grad = lax.optimization_barrier((back[0], row_grad))
    back.append(
        lax.all_to_all(row_grad.reshape(experts, sizes[1], width), "expert", 0, 0, tiled=True)
    )
    returned = jnp.concatenate(
        [back[0].reshape(experts * sizes[0], width), back[1].reshape(experts * sizes[1], width)],
        axis=0,
    )
    grad_w_out, grad_w_in = [keep + got.astype(jnp.float32) for keep, got in finals]

    grad_latents = lax.dot_general(
        table, returned, (((0,), (0,)), ((), ())), preferred_element_type=jnp.float32
    )
    grad_latents = grad_latents.astype(jnp.bfloat16)
    return (grad_latents, grad_w_in[None], grad_w_out[None])


def solution(mesh):
    return _sharded(mesh)


def _sharded(mesh):
    return jax.shard_map(
        per_device,
        mesh=mesh,
        in_specs=(
            P(("dp", "expert"), None),
            P(("dp", "expert"), None),
            P(("dp", "expert")),
            P("expert", None, None),
            P("expert", None, None),
        ),
        out_specs=(P(("dp", "expert"), None), P("expert", "dp", None), P("expert", "dp", None)),
        check_vma=False,
    )
```
